256 devices in a mesh: wide: 32 (over x, y, core), blk: 8 (over z).
Axes of the slice: x: 4, y: 4, z: 8, core: 2. Of those that a mesh axis runs over, the one named last changes fastest.
Arguments:
- tokens: bfloat16 [1024, 8192], P('wide', 'blk'), may hold values from -6 to 6
- target: bfloat16 [1024, 8192], P('wide', 'blk'), may hold values from -3 to 3
- probe_vector: float32 [8192], P('blk'), may hold values from -12 to 12
- weight_in: bfloat16 [256, 8, 2, 128, 128], P('wide', 'blk'), may hold values from -0.375 to 0.375
- weight_out: bfloat16 [256, 8, 2, 128, 128], P('wide', 'blk'), may hold values from -0.09375 to 0.09375
- slot_rows: int32 [256, 8, 2], P('wide', 'blk'), may hold values from 0 to 7, as said below
- slot_count: int32 [256, 8], P('wide', 'blk'), may hold values from 0 to 2, as said below
Outputs:
- outputs: bfloat16 [1024, 8192], P('wide', 'blk')
- token_grad: bfloat16 [1024, 8192], P('wide', 'blk')
- grad_in: float32 [256, 8, 2, 128, 128], P('wide', 'blk')
- grad_out: float32 [256, 8, 2, 128, 128], P('wide', 'blk')
The draws below stay inside these ranges and needn't reach their ends.
Inputs may be any that keep to these rules, and one draw needn't show every extreme that they name: `slot_rows`: the 2 entries of one (j, g) are distinct feature blocks of the row group. `slot_count`: every hidden block column has 2 used slots in at least one row group.
All inputs are finite; a program needn't handle non-finite values.
Results may differ from the reference program's by a relative error of at most 0.033.
Values may be sent and summed in bfloat16 or wider, within the bound.
No kernel may reach another device: no remote copies, remote signals or barrier semaphores. Data moves between devices by JAX's collectives and lax.ppermute only.
A program may use at most 64 MiB of HBM per device.

```python
import jax
import jax.numpy as jnp
from jax import lax

D = 8192
H = 32768
BLK = 128
CAP = 2
TOKENS = 1024
HB = 256
RG = 8
RBG = 8
N_WIDE = 32


def draw_probe_vector(key, part):
    position = jnp.arange(D, dtype=jnp.float32) / max(D - 1, 1)
    rising = 1.0 + 2.0 * position
    base = jnp.clip(jax.random.normal(key, (D,), jnp.float32), -4.0, 4.0)
    return base * rising


def draw_weight_in(key, part):
    shape = (HB, RG, CAP, BLK, BLK)
    column = jnp.arange(HB, dtype=jnp.float32).reshape(HB, 1, 1, 1, 1) / max(HB - 1, 1)
    rising = (1.0 + 2.0 * column) / (D // 8) ** 0.5
    base = jnp.clip(jax.random.normal(key, shape, jnp.float32), -4.0, 4.0)
    return (base * rising).astype(jnp.bfloat16)


def draw_slot_rows(key, part):
    scores = jax.random.randint(key, (HB, RG, RBG), 0, 1 << 20) * RBG + jnp.arange(RBG, dtype=jnp.int32)
    order = jnp.argsort(scores, axis=-1)
    return order[:, :, :CAP].astype(jnp.int32)


def draw_slot_count(key, part):
    first_key, second_key = jax.random.split(key)
    levels = jax.random.randint(first_key, (HB, RG), 0, CAP + 1)
    filled = jax.random.randint(second_key, (HB, 1), 0, RG)
    groups = jnp.arange(RG, dtype=jnp.int32)[None, :]
    return jnp.where(groups == filled, CAP, levels).astype(jnp.int32)


def shard_levels(own_key, extent, cuts, low, high):
    def one(dim, blocks):
        draws = jax.random.uniform(jax.random.fold_in(jax.random.fold_in(own_key, 6), dim), (blocks,), jnp.float32, low / len(cuts), high / len(cuts))
        return jnp.repeat(jnp.exp(draws), extent[dim] // blocks).reshape((-1,) + (1,) * (len(extent) - dim - 1))

    gain = one(*cuts[0])
    for cut in cuts[1:]:
        gain = gain * one(*cut)
    return gain


def centred(own_key, dims, scale, reach, cuts=(), kind=jnp.bfloat16):
    values = jax.random.normal(own_key, dims, jnp.float32) * scale
    if len(cuts) > 0:
        values = shard_levels(own_key, dims, cuts, -0.22, 0.18) * values
    return jnp.clip(values, min=-reach, max=reach).astype(kind)


def setup_inputs(seed: int = 0) -> dict:
    arg_keys = jax.random.split(jax.random.key(seed), 8)
    return {
        "tokens": centred(arg_keys[0], (TOKENS, D), 1.0, 6.0, ((0, 32), (1, 8))),
        "target": centred(arg_keys[1], (TOKENS, D), 0.5, 3.0, ((0, 32), (1, 8))),
        "probe_vector": draw_probe_vector(jax.random.fold_in(arg_keys[7], 71), 0),
        "weight_in": draw_weight_in(jax.random.fold_in(arg_keys[7], 71), 0),
        "weight_out": centred(arg_keys[4], (HB, RG, CAP, BLK, BLK), (H // 8) ** -0.5, 0.09375, ((0, 32), (1, 8))),
        "slot_rows": draw_slot_rows(jax.random.fold_in(arg_keys[7], 71), 0),
        "slot_count": draw_slot_count(jax.random.fold_in(arg_keys[7], 71), 0),
    }


def activate(value):
    return jax.nn.gelu(value, approximate=True)

def activate_slope(value):
    return jax.jvp(activate, (value,), (jnp.ones_like(value),))[1]

def rounded(value):
    lowered = lax.optimization_barrier(value.astype(jnp.bfloat16))
    return lowered.astype(jnp.float32)

def pick_rows(blocks, row_index):
    group = lax.broadcasted_iota(jnp.int32, row_index.shape, 1)
    return blocks[:, group, row_index, :]

def place_rows(contrib, row_index):
    onehot = (row_index[..., None] == lax.broadcasted_iota(jnp.int32, row_index.shape + (RBG,), 3)).astype(jnp.float32)
    placed = jnp.einsum('tjgsn,jgsr->tgrn', contrib, onehot)
    return placed.reshape(contrib.shape[0], D)

def reference(tokens, target, probe_vector, weight_in, weight_out, slot_rows, slot_count):
    in_use = lax.broadcasted_iota(jnp.int32, slot_rows.shape, 2) < slot_count[:, :, None]
    mask = in_use.astype(jnp.float32)[..., None, None]
    tiles_in = weight_in.astype(jnp.float32) * mask
    tiles_out = weight_out.astype(jnp.float32) * mask
    inputs = tokens.astype(jnp.float32).reshape(TOKENS, RG, RBG, BLK)
    chosen = pick_rows(probe_vector.reshape(1, RG, RBG, BLK), slot_rows)[0]
    image = jnp.einsum('jgsk,jgskn->jn', chosen, tiles_in, precision=lax.Precision.HIGHEST)
    norm_probe = jnp.sum(probe_vector * probe_vector)
    spectral = jnp.sqrt(jnp.sum(image * image) / norm_probe)
    per_group = HB // N_WIDE

    def grouped(array):
        return array.reshape((N_WIDE, per_group) + array.shape[1:])
    items = (grouped(tiles_in), grouped(tiles_out), grouped(slot_rows))

    def hidden_of(tile_group, row_group):
        picked = pick_rows(inputs, row_group)
        return jnp.einsum('tjgsk,jgskn->tjn', picked, tile_group) / spectral

    def forward_group(carry, item):
        tile_group, out_group, row_group = item
        hidden = hidden_of(tile_group, row_group)
        active = rounded(activate(hidden))
        contrib = jnp.einsum('tjk,jgskn->tjgsn', active, out_group)
        return (carry + rounded(place_rows(contrib, row_group)), None)
    summed, unused = lax.scan(forward_group, jnp.zeros((TOKENS, D), jnp.float32), items)
    outputs = summed.astype(jnp.bfloat16)
    residual = (outputs.astype(jnp.float32) - target.astype(jnp.float32)).astype(jnp.bfloat16)
    errors = residual.astype(jnp.float32).reshape(TOKENS, RG, RBG, BLK)

    def backward_group(carry, item):
        tile_group, out_group, row_group = item
        hidden = hidden_of(tile_group, row_group)
        active = rounded(activate(hidden))
        picked_err = pick_rows(errors, row_group)
        back = jnp.einsum('tjgsn,jgskn->tjk', picked_err, out_group)
        slope = rounded(back * activate_slope(hidden))
        part_out = jnp.einsum('tjk,tjgsn->jgskn', active, picked_err)
        picked_in = pick_rows(inputs, row_group)
        part_in = jnp.einsum('tjgsk,tjn->jgskn', picked_in, slope)
        spread = jnp.einsum('tjn,jgskn->tjgsk', slope, tile_group)
        return (carry + rounded(place_rows(spread, row_group)), (part_in, part_out))
    back_sum, stacked = lax.scan(backward_group, jnp.zeros((TOKENS, D), jnp.float32), items)
    raw_in = stacked[0].reshape(HB, RG, CAP, BLK, BLK) * mask
    grad_out = stacked[1].reshape(HB, RG, CAP, BLK, BLK) * mask
    curvature = jnp.sum(raw_in * tiles_in)
    outer = jnp.einsum('jgsk,jn->jgskn', chosen, image) * mask
    grad_in = raw_in / spectral - curvature / (spectral ** 3 * norm_probe) * outer
    token_grad = (back_sum / spectral).astype(jnp.bfloat16)
    return (outputs, token_grad, grad_in, grad_out)
```

```python
import jax
import jax.numpy as jnp
from jax import lax
from jax.sharding import PartitionSpec as P


def activate(value):
    return jax.nn.gelu(value, approximate=True)


def activate_slope(value):
    return jax.jvp(activate, (value,), (jnp.ones_like(value),))[1]


def spread_tiles(tiles, row_index, feature_blocks):
    rows = lax.broadcasted_iota(jnp.int32, (feature_blocks,) + row_index.shape, 0)
    hit = rows == row_index[None]
    zero = jnp.zeros((), tiles.dtype)
    dense = jnp.where(hit[:, :, 0, None, None], tiles[None, :, 0], zero)
    for slot in range(1, row_index.shape[1]):
        dense = dense + jnp.where(hit[:, :, slot, None, None], tiles[None, :, slot], zero)
    return jnp.transpose(dense, (0, 2, 1, 3))


def pick_tiles(dense, row_index):
    feature_blocks = dense.shape[0]
    rows = lax.broadcasted_iota(jnp.int32, (feature_blocks,) + row_index.shape, 0)
    hit = rows == row_index[None]
    by_col = jnp.transpose(dense, (0, 2, 1, 3))
    picked = jnp.zeros(row_index.shape + dense.shape[1:2] + dense.shape[3:4], dense.dtype)
    for r in range(feature_blocks):
        picked = picked + jnp.where(hit[r][:, :, None, None], by_col[r][:, None], 0.0)
    return picked


def body(tokens, target, probe_vector, weight_in, weight_out, slot_rows, slot_count):
    columns, unit, slots, block, width_two = weight_in.shape
    features = tokens.shape[1]
    feature_blocks = features // block
    hidden_width = columns * block
    row_index = slot_rows[:, 0]
    in_use = lax.broadcasted_iota(jnp.int32, (columns, slots), 1) < slot_count[:, 0][:, None]
    mask_low = in_use.astype(jnp.bfloat16)[:, :, None, None]
    mask_full = in_use.astype(jnp.float32)[:, :, None, None]
    tiles_in = weight_in[:, 0] * mask_low
    tiles_out = weight_out[:, 0] * mask_low
    chosen = jnp.take(
        probe_vector.reshape(feature_blocks, block), row_index.reshape(-1), axis=0
    ).reshape(columns, slots, block)
    image_part = jnp.einsum(
        "jsk,jskn->jn", chosen, tiles_in.astype(jnp.float32), precision=lax.Precision.HIGHEST
    )
    image, norm_probe = lax.psum((image_part, jnp.sum(probe_vector * probe_vector)), "blk")
    norm_image = lax.psum(jnp.sum(image * image), "wide")
    spectral = jnp.sqrt(norm_image / norm_probe)

    w1 = spread_tiles(tiles_in, row_index, feature_blocks).reshape(features, hidden_width)
    w2 = jnp.transpose(
        spread_tiles(tiles_out, row_index, feature_blocks), (2, 1, 0, 3)
    ).reshape(hidden_width, features)

    x_full = lax.all_gather(tokens, "wide", axis=0, tiled=True)
    x_full, spectral = lax.optimization_barrier((x_full, spectral))

    pre_part = jnp.dot(x_full, w1, preferred_element_type=jnp.float32)
    pre_own = lax.psum_scatter(
        pre_part.astype(jnp.bfloat16), "blk", scatter_dimension=0, tiled=True
    ).astype(jnp.float32)
    hidden_own = pre_own / spectral
    active_own = activate(hidden_own).astype(jnp.bfloat16)
    active_full = lax.all_gather(active_own, "blk", axis=0, tiled=True)

    out_part = jnp.dot(active_full, w2, preferred_element_type=jnp.float32)
    outputs = lax.psum_scatter(
        out_part.astype(jnp.bfloat16), "wide", scatter_dimension=0, tiled=True
    )
    residual = (outputs.astype(jnp.float32) - target.astype(jnp.float32)).astype(jnp.bfloat16)
    error_full = lax.all_gather(residual, "wide", axis=0, tiled=True)

    back_part = lax.dot_general(
        error_full, w2, (((1,), (1,)), ((), ())), preferred_element_type=jnp.float32
    )
    back_own = lax.psum_scatter(
        back_part.astype(jnp.bfloat16), "blk", scatter_dimension=0, tiled=True
    ).astype(jnp.float32)
    slope_own = (back_own * activate_slope(hidden_own)).astype(jnp.bfloat16)
    curvature = lax.psum(jnp.sum(slope_own.astype(jnp.float32) * pre_own), ("wide", "blk"))
    slope_full = lax.all_gather(slope_own, "blk", axis=0, tiled=True)

    in_part = lax.dot_general(
        slope_full, w1, (((1,), (1,)), ((), ())), preferred_element_type=jnp.float32
    )
    token_grad = (
        lax.psum_scatter(in_part.astype(jnp.bfloat16), "wide", scatter_dimension=0, tiled=True)
        .astype(jnp.float32)
        / spectral
    ).astype(jnp.bfloat16)

    g1 = lax.dot_general(
        x_full, slope_full, (((0,), (0,)), ((), ())), preferred_element_type=jnp.float32
    )
    raw_in = pick_tiles(g1.reshape(feature_blocks, block, columns, block), row_index) * mask_full
    g2 = lax.dot_general(
        error_full, active_full, (((0,), (0,)), ((), ())), preferred_element_type=jnp.float32
    )
    grad_out = pick_tiles(g2.reshape(feature_blocks, block, columns, block), row_index) * mask_full
    grad_out = jnp.transpose(grad_out, (0, 1, 3, 2))

    outer = jnp.einsum("jsk,jn->jskn", chosen, image) * mask_full
    grad_in = raw_in / spectral - curvature / (spectral**3 * norm_probe) * outer
    return (outputs, token_grad, grad_in[:, None], grad_out[:, None])


def solution(mesh):
    in_specs = (
        P("wide", "blk"),
        P("wide", "blk"),
        P("blk"),
        P("wide", "blk", None, None, None),
        P("wide", "blk", None, None, None),
        P("wide", "blk", None),
        P("wide", "blk"),
    )
    out_specs = (
        P("wide", "blk"),
        P("wide", "blk"),
        P("wide", "blk", None, None, None),
        P("wide", "blk", None, None, None),
    )
    return jax.shard_map(body, mesh=mesh, in_specs=in_specs, out_specs=out_specs, check_vma=False)
```

```python
import jax
import jax.numpy as jnp
from jax import lax
from jax.sharding import PartitionSpec as P


def activate(value):
    return jax.nn.gelu(value, approximate=True)


def activate_slope(value):
    return jax.jvp(activate, (value,), (jnp.ones_like(value),))[1]


def spread_tiles(tiles, row_index, feature_blocks):
    rows = lax.broadcasted_iota(jnp.int32, (feature_blocks,) + row_index.shape, 0)
    hit = rows == row_index[None]
    zero = jnp.zeros((), tiles.dtype)
    dense = jnp.where(hit[:, :, 0, None, None], tiles[None, :, 0], zero)
    for slot in range(1, row_index.shape[1]):
        dense = dense + jnp.where(hit[:, :, slot, None, None], tiles[None, :, slot], zero)
    return jnp.transpose(dense, (0, 2, 1, 3))


def pick_tiles(dense, row_index):
    feature_blocks = dense.shape[0]
    rows = lax.broadcasted_iota(jnp.int32, (feature_blocks,) + row_index.shape, 0)
    hit = rows == row_index[None]
    by_col = jnp.transpose(dense, (0, 2, 1, 3))
    picked = jnp.zeros(row_index.shape + dense.shape[1:2] + dense.shape[3:4], dense.dtype)
    for r in range(feature_blocks):
        picked = picked + jnp.where(hit[r][:, :, None, None], by_col[r][:, None], 0.0)
    return picked


def butterfly_sum(value, axis):
    size = lax.axis_size(axis)
    step = 1
    while step < size:
        value = value + lax.ppermute(value, axis, [(i, i ^ step) for i in range(size)])
        step *= 2
    return value


def body(tokens, target, probe_vector, weight_in, weight_out, slot_rows, slot_count):
    columns, unit, slots, block, width_two = weight_in.shape
    features = tokens.shape[1]
    feature_blocks = features // block
    hidden_width = columns * block
    row_index = slot_rows[:, 0]
    in_use = lax.broadcasted_iota(jnp.int32, (columns, slots), 1) < slot_count[:, 0][:, None]
    mask_low = in_use.astype(jnp.bfloat16)[:, :, None, None]
    mask_full = in_use.astype(jnp.float32)[:, :, None, None]
    tiles_in = weight_in[:, 0] * mask_low
    tiles_out = weight_out[:, 0] * mask_low
    chosen = jnp.take(
        probe_vector.reshape(feature_blocks, block), row_index.reshape(-1), axis=0
    ).reshape(columns, slots, block)
    image_part = jnp.einsum(
        "jsk,jskn->jn", chosen, tiles_in.astype(jnp.float32), precision=lax.Precision.HIGHEST
    )
    image_and_norm = butterfly_sum(
        jnp.concatenate([image_part.reshape(-1), jnp.sum(probe_vector * probe_vector)[None]]), "blk"
    )
    image = image_and_norm[:-1].reshape(image_part.shape)
    norm_probe = image_and_norm[-1]
    norm_image = butterfly_sum(jnp.sum(image * image)[None], "wide")[0]
    spectral = jnp.sqrt(norm_image / norm_probe)

    w1 = spread_tiles(tiles_in, row_index, feature_blocks).reshape(features, hidden_width)
    w2 = jnp.transpose(
        spread_tiles(tiles_out, row_index, feature_blocks), (2, 1, 0, 3)
    ).reshape(hidden_width, features)

    x_full = lax.all_gather(tokens, "wide", axis=0, tiled=True)
    x_full, spectral = lax.optimization_barrier((x_full, spectral))

    pre_part = jnp.dot(x_full, w1, preferred_element_type=jnp.float32)
    pre_own = lax.psum_scatter(
        pre_part.astype(jnp.bfloat16), "blk", scatter_dimension=0, tiled=True
    ).astype(jnp.float32)
    hidden_own = pre_own / spectral
    active_own = activate(hidden_own).astype(jnp.bfloat16)
    active_full = lax.all_gather(active_own, "blk", axis=0, tiled=True)

    out_part = jnp.dot(active_full, w2, preferred_element_type=jnp.float32)
    outputs = lax.psum_scatter(
        out_part.astype(jnp.bfloat16), "wide", scatter_dimension=0, tiled=True
    )
    residual = (outputs.astype(jnp.float32) - target.astype(jnp.float32)).astype(jnp.bfloat16)
    error_full = lax.all_gather(residual, "wide", axis=0, tiled=True)

    back_part = lax.dot_general(
        error_full, w2, (((1,), (1,)), ((), ())), preferred_element_type=jnp.float32
    )
    back_own = lax.psum_scatter(
        back_part.astype(jnp.bfloat16), "blk", scatter_dimension=0, tiled=True
    ).astype(jnp.float32)
    slope_own = (back_own * activate_slope(hidden_own)).astype(jnp.bfloat16)
    curvature = butterfly_sum(
        butterfly_sum(jnp.sum(slope_own.astype(jnp.float32) * pre_own)[None], "blk"), "wide"
    )[0]
    slope_full = lax.all_gather(slope_own, "blk", axis=0, tiled=True)

    in_part = lax.dot_general(
        slope_full, w1, (((1,), (1,)), ((), ())), preferred_element_type=jnp.float32
    )
    token_grad = (
        lax.psum_scatter(in_part.astype(jnp.bfloat16), "wide", scatter_dimension=0, tiled=True)
        .astype(jnp.float32)
        / spectral
    ).astype(jnp.bfloat16)

    g1 = lax.dot_general(
        x_full, slope_full, (((0,), (0,)), ((), ())), preferred_element_type=jnp.float32
    )
    raw_in = pick_tiles(g1.reshape(feature_blocks, block, columns, block), row_index) * mask_full
    g2 = lax.dot_general(
        error_full, active_full, (((0,), (0,)), ((), ())), preferred_element_type=jnp.float32
    )
    grad_out = pick_tiles(g2.reshape(feature_blocks, block, columns, block), row_index) * mask_full
    grad_out = jnp.transpose(grad_out, (0, 1, 3, 2))

    outer = jnp.einsum("jsk,jn->jskn", chosen, image) * mask_full
    grad_in = raw_in / spectral - curvature / (spectral**3 * norm_probe) * outer
    return (outputs, token_grad, grad_in[:, None], grad_out[:, None])


def solution(mesh):
    in_specs = (
        P("wide", "blk"),
        P("wide", "blk"),
        P("blk"),
        P("wide", "blk", None, None, None),
        P("wide", "blk", None, None, None),
        P("wide", "blk", None),
        P("wide", "blk"),
    )
    out_specs = (
        P("wide", "blk"),
        P("wide", "blk"),
        P("wide", "blk", None, None, None),
        P("wide", "blk", None, None, None),
    )
    return jax.shard_map(body, mesh=mesh, in_specs=in_specs, out_specs=out_specs, check_vma=False)
```

```python
import jax
import jax.numpy as jnp
from jax import lax
from jax.sharding import PartitionSpec as P


def activate(value):
    return jax.nn.gelu(value, approximate=True)


def activate_slope(value):
    return jax.jvp(activate, (value,), (jnp.ones_like(value),))[1]


def spread_tiles(tiles, row_index, feature_blocks):
    rows = lax.broadcasted_iota(jnp.int32, (feature_blocks,) + row_index.shape, 0)
    hit = rows == row_index[None]
    zero = jnp.zeros((), tiles.dtype)
    dense = jnp.where(hit[:, :, 0, None, None], tiles[None, :, 0], zero)
    for slot in range(1, row_index.shape[1]):
        dense = dense + jnp.where(hit[:, :, slot, None, None], tiles[None, :, slot], zero)
    return jnp.transpose(dense, (0, 2, 1, 3))


def pick_tiles(dense, row_index):
    feature_blocks = dense.shape[0]
    rows = lax.broadcasted_iota(jnp.int32, (feature_blocks,) + row_index.shape, 0)
    hit = rows == row_index[None]
    by_col = jnp.transpose(dense, (0, 2, 1, 3))
    picked = jnp.zeros(row_index.shape + dense.shape[1:2] + dense.shape[3:4], dense.dtype)
    for r in range(feature_blocks):
        picked = picked + jnp.where(hit[r][:, :, None, None], by_col[r][:, None], 0.0)
    return picked


def butterfly_sum(value, axis):
    size = lax.axis_size(axis)
    step = 1
    while step < size:
        value = value + lax.ppermute(value, axis, [(i, i ^ step) for i in range(size)])
        step *= 2
    return value


def gather_rows(value, axis):
    size = lax.axis_size(axis)
    spread = jnp.broadcast_to(value[None], (size,) + value.shape)
    gathered = lax.all_to_all(spread, axis, 0, 0, tiled=False)
    return gathered.reshape((size * value.shape[0],) + value.shape[1:])


def sum_rows(value, axis):
    size = lax.axis_size(axis)
    parts = value.reshape((size, value.shape[0] // size) + value.shape[1:])
    received = lax.all_to_all(parts, axis, 0, 0, tiled=False)
    return jnp.sum(received.astype(jnp.float32), axis=0)


def body(tokens, target, probe_vector, weight_in, weight_out, slot_rows, slot_count):
    columns, unit, slots, block, width_two = weight_in.shape
    features = tokens.shape[1]
    feature_blocks = features // block
    hidden_width = columns * block
    row_index = slot_rows[:, 0]
    in_use = lax.broadcasted_iota(jnp.int32, (columns, slots), 1) < slot_count[:, 0][:, None]
    mask_low = in_use.astype(jnp.bfloat16)[:, :, None, None]
    mask_full = in_use.astype(jnp.float32)[:, :, None, None]
    tiles_in = weight_in[:, 0] * mask_low
    tiles_out = weight_out[:, 0] * mask_low
    chosen = jnp.take(
        probe_vector.reshape(feature_blocks, block), row_index.reshape(-1), axis=0
    ).reshape(columns, slots, block)
    image_part = jnp.einsum(
        "jsk,jskn->jn", chosen, tiles_in.astype(jnp.float32), precision=lax.Precision.HIGHEST
    )
    image_and_norm = butterfly_sum(
        jnp.concatenate([image_part.reshape(-1), jnp.sum(probe_vector * probe_vector)[None]]), "blk"
    )
    image = image_and_norm[:-1].reshape(image_part.shape)
    norm_probe = image_and_norm[-1]
    norm_image = butterfly_sum(jnp.sum(image * image)[None], "wide")[0]
    spectral = jnp.sqrt(norm_image / norm_probe)

    w1 = spread_tiles(tiles_in, row_index, feature_blocks).reshape(features, hidden_width)
    w2 = jnp.transpose(
        spread_tiles(tiles_out, row_index, feature_blocks), (2, 1, 0, 3)
    ).reshape(hidden_width, features)

    x_full = gather_rows(tokens, "wide")
    x_full, spectral = lax.optimization_barrier((x_full, spectral))

    pre_part = jnp.dot(x_full, w1, preferred_element_type=jnp.float32)
    pre_own = lax.psum_scatter(
        pre_part.astype(jnp.bfloat16), "blk", scatter_dimension=0, tiled=True
    ).astype(jnp.float32)
    hidden_own = pre_own / spectral
    active_own = activate(hidden_own).astype(jnp.bfloat16)
    active_full = lax.all_gather(active_own, "blk", axis=0, tiled=True)

    out_part = jnp.dot(active_full, w2, preferred_element_type=jnp.float32)
    outputs = sum_rows(out_part.astype(jnp.bfloat16), "wide").astype(jnp.bfloat16)
    residual = (outputs.astype(jnp.float32) - target.astype(jnp.float32)).astype(jnp.bfloat16)
    error_full = gather_rows(residual, "wide")

    back_part = lax.dot_general(
        error_full, w2, (((1,), (1,)), ((), ())), preferred_element_type=jnp.float32
    )
    back_own = lax.psum_scatter(
        back_part.astype(jnp.bfloat16), "blk", scatter_dimension=0, tiled=True
    ).astype(jnp.float32)
    slope_own = (back_own * activate_slope(hidden_own)).astype(jnp.bfloat16)
    curvature = butterfly_sum(
        butterfly_sum(jnp.sum(slope_own.astype(jnp.float32) * pre_own)[None], "blk"), "wide"
    )[0]
    slope_full = lax.all_gather(slope_own, "blk", axis=0, tiled=True)

    in_part = lax.dot_general(
        slope_full, w1, (((1,), (1,)), ((), ())), preferred_element_type=jnp.float32
    )
    token_grad = (sum_rows(in_part.astype(jnp.bfloat16), "wide") / spectral).astype(jnp.bfloat16)

    g1 = lax.dot_general(
        x_full, slope_full, (((0,), (0,)), ((), ())), preferred_element_type=jnp.float32
    )
    raw_in = pick_tiles(g1.reshape(feature_blocks, block, columns, block), row_index) * mask_full
    g2 = lax.dot_general(
        error_full, active_full, (((0,), (0,)), ((), ())), preferred_element_type=jnp.float32
    )
    grad_out = pick_tiles(g2.reshape(feature_blocks, block, columns, block), row_index) * mask_full
    grad_out = jnp.transpose(grad_out, (0, 1, 3, 2))

    outer = jnp.einsum("jsk,jn->jskn", chosen, image) * mask_full
    grad_in = raw_in / spectral - curvature / (spectral**3 * norm_probe) * outer
    return (outputs, token_grad, grad_in[:, None], grad_out[:, None])


def solution(mesh):
    in_specs = (
        P("wide", "blk"),
        P("wide", "blk"),
        P("blk"),
        P("wide", "blk", None, None, None),
        P("wide", "blk", None, None, None),
        P("wide", "blk", None),
        P("wide", "blk"),
    )
    out_specs = (
        P("wide", "blk"),
        P("wide", "blk"),
        P("wide", "blk", None, None, None),
        P("wide", "blk", None, None, None),
    )
    return jax.shard_map(body, mesh=mesh, in_specs=in_specs, out_specs=out_specs, check_vma=False)
```

```python
import jax
import jax.numpy as jnp
from jax import lax
from jax.sharding import PartitionSpec as P


def activate(value):
    return jax.nn.gelu(value, approximate=True)


def activate_slope(value):
    return jax.jvp(activate, (value,), (jnp.ones_like(value),))[1]


def spread_tiles(tiles, row_index, feature_blocks):
    rows = lax.broadcasted_iota(jnp.int32, (feature_blocks,) + row_index.shape, 0)
    hit = rows == row_index[None]
    zero = jnp.zeros((), tiles.dtype)
    dense = jnp.where(hit[:, :, 0, None, None], tiles[None, :, 0], zero)
    for slot in range(1, row_index.shape[1]):
        dense = dense + jnp.where(hit[:, :, slot, None, None], tiles[None, :, slot], zero)
    return jnp.transpose(dense, (0, 2, 1, 3))


def pick_tiles(dense, row_index):
    feature_blocks = dense.shape[0]
    rows = lax.broadcasted_iota(jnp.int32, (feature_blocks,) + row_index.shape, 0)
    hit = rows == row_index[None]
    by_col = jnp.transpose(dense, (0, 2, 1, 3))
    picked = jnp.zeros(row_index.shape + dense.shape[1:2] + dense.shape[3:4], dense.dtype)
    for r in range(feature_blocks):
        picked = picked + jnp.where(hit[r][:, :, None, None], by_col[r][:, None], 0.0)
    return picked


def butterfly_sum(value, axis):
    size = lax.axis_size(axis)
    step = 1
    while step < size:
        value = value + lax.ppermute(value, axis, [(i, i ^ step) for i in range(size)])
        step *= 2
    return value


def gather_rows(value, axis):
    size = lax.axis_size(axis)
    spread = jnp.broadcast_to(value[None], (size,) + value.shape)
    gathered = lax.all_to_all(spread, axis, 0, 0, tiled=False)
    return gathered.reshape((size * value.shape[0],) + value.shape[1:])


def sum_rows(value, axis):
    size = lax.axis_size(axis)
    parts = value.reshape((size, value.shape[0] // size) + value.shape[1:])
    received = lax.all_to_all(parts, axis, 0, 0, tiled=False)
    return jnp.sum(received.astype(jnp.float32), axis=0)


def body(tokens, target, probe_vector, weight_in, weight_out, slot_rows, slot_count):
    columns, unit, slots, block, width_two = weight_in.shape
    features = tokens.shape[1]
    feature_blocks = features // block
    hidden_width = columns * block
    row_index = slot_rows[:, 0]
    in_use = lax.broadcasted_iota(jnp.int32, (columns, slots), 1) < slot_count[:, 0][:, None]
    mask_low = in_use.astype(jnp.bfloat16)[:, :, None, None]
    mask_full = in_use.astype(jnp.float32)[:, :, None, None]
    tiles_in = weight_in[:, 0] * mask_low
    tiles_out = weight_out[:, 0] * mask_low
    chosen = jnp.take(
        probe_vector.reshape(feature_blocks, block), row_index.reshape(-1), axis=0
    ).reshape(columns, slots, block)
    image_part = jnp.einsum(
        "jsk,jskn->jn", chosen, tiles_in.astype(jnp.float32), precision=lax.Precision.HIGHEST
    )
    image_and_norm = butterfly_sum(
        jnp.concatenate([image_part.reshape(-1), jnp.sum(probe_vector * probe_vector)[None]]), "blk"
    )
    image = image_and_norm[:-1].reshape(image_part.shape)
    norm_probe = image_and_norm[-1]
    norm_image = butterfly_sum(jnp.sum(image * image)[None], "wide")[0]
    spectral = jnp.sqrt(norm_image / norm_probe)

    w1 = spread_tiles(tiles_in, row_index, feature_blocks).reshape(features, hidden_width)
    w2 = jnp.transpose(
        spread_tiles(tiles_out, row_index, feature_blocks), (2, 1, 0, 3)
    ).reshape(hidden_width, features)

    x_full = gather_rows(tokens, "wide")
    pre_part = jnp.dot(x_full, w1, preferred_element_type=jnp.float32)
    pre_own = lax.psum_scatter(
        pre_part.astype(jnp.bfloat16), "blk", scatter_dimension=0, tiled=True
    ).astype(jnp.float32)
    pre_own, spectral = lax.optimization_barrier((pre_own, spectral))
    hidden_own = pre_own / spectral
    active_own = activate(hidden_own).astype(jnp.bfloat16)
    active_full = lax.all_gather(active_own, "blk", axis=0, tiled=True)

    out_part = jnp.dot(active_full, w2, preferred_element_type=jnp.float32)
    outputs = sum_rows(out_part.astype(jnp.bfloat16), "wide").astype(jnp.bfloat16)
    residual = (outputs.astype(jnp.float32) - target.astype(jnp.float32)).astype(jnp.bfloat16)
    error_full = gather_rows(residual, "wide")

    back_part = lax.dot_general(
        error_full, w2, (((1,), (1,)), ((), ())), preferred_element_type=jnp.float32
    )
    back_own = lax.psum_scatter(
        back_part.astype(jnp.bfloat16), "blk", scatter_dimension=0, tiled=True
    ).astype(jnp.float32)
    slope_own = (back_own * activate_slope(hidden_own)).astype(jnp.bfloat16)
    curvature = butterfly_sum(
        butterfly_sum(jnp.sum(slope_own.astype(jnp.float32) * pre_own)[None], "blk"), "wide"
    )[0]
    slope_full = lax.all_gather(slope_own, "blk", axis=0, tiled=True)
    slope_full, curvature = lax.optimization_barrier((slope_full, curvature))

    in_part = lax.dot_general(
        slope_full, w1, (((1,), (1,)), ((), ())), preferred_element_type=jnp.float32
    )
    token_grad = (sum_rows(in_part.astype(jnp.bfloat16), "wide") / spectral).astype(jnp.bfloat16)

    g1 = lax.dot_general(
        x_full, slope_full, (((0,), (0,)), ((), ())), preferred_element_type=jnp.float32
    )
    raw_in = pick_tiles(g1.reshape(feature_blocks, block, columns, block), row_index) * mask_full
    g2 = lax.dot_general(
        error_full, active_full, (((0,), (0,)), ((), ())), preferred_element_type=jnp.float32
    )
    grad_out = pick_tiles(g2.reshape(feature_blocks, block, columns, block), row_index) * mask_full
    grad_out = jnp.transpose(grad_out, (0, 1, 3, 2))

    outer = jnp.einsum("jsk,jn->jskn", chosen, image) * mask_full
    grad_in = raw_in / spectral - curvature / (spectral**3 * norm_probe) * outer
    return (outputs, token_grad, grad_in[:, None], grad_out[:, None])


def solution(mesh):
    in_specs = (
        P("wide", "blk"),
        P("wide", "blk"),
        P("blk"),
        P("wide", "blk", None, None, None),
        P("wide", "blk", None, None, None),
        P("wide", "blk", None),
        P("wide", "blk"),
    )
    out_specs = (
        P("wide", "blk"),
        P("wide", "blk"),
        P("wide", "blk", None, None, None),
        P("wide", "blk", None, None, None),
    )
    return jax.shard_map(body, mesh=mesh, in_specs=in_specs, out_specs=out_specs, check_vma=False)
```

```python
import jax
import jax.numpy as jnp
from jax import lax
from jax.sharding import PartitionSpec as P


def activate(value):
    return jax.nn.gelu(value, approximate=True)


def activate_slope(value):
    return jax.jvp(activate, (value,), (jnp.ones_like(value),))[1]


def spread_tiles(tiles, row_index, feature_blocks):
    rows = lax.broadcasted_iota(jnp.int32, (feature_blocks,) + row_index.shape, 0)
    hit = rows == row_index[None]
    zero = jnp.zeros((), tiles.dtype)
    dense = jnp.where(hit[:, :, 0, None, None], tiles[None, :, 0], zero)
    for slot in range(1, row_index.shape[1]):
        dense = dense + jnp.where(hit[:, :, slot, None, None], tiles[None, :, slot], zero)
    return jnp.transpose(dense, (0, 2, 1, 3))


def pick_tiles(dense, row_index):
    feature_blocks = dense.shape[0]
    rows = lax.broadcasted_iota(jnp.int32, (feature_blocks,) + row_index.shape, 0)
    hit = rows == row_index[None]
    by_col = jnp.transpose(dense, (0, 2, 1, 3))
    picked = jnp.zeros(row_index.shape + dense.shape[1:2] + dense.shape[3:4], dense.dtype)
    for r in range(feature_blocks):
        picked = picked + jnp.where(hit[r][:, :, None, None], by_col[r][:, None], 0.0)
    return picked


def butterfly_sum(value, axis):
    size = lax.axis_size(axis)
    step = 1
    while step < size:
        value = value + lax.ppermute(value, axis, [(i, i ^ step) for i in range(size)])
        step *= 2
    return value


def gather_rows(value, axis):
    size = lax.axis_size(axis)
    spread = jnp.broadcast_to(value[None], (size,) + value.shape)
    gathered = lax.all_to_all(spread, axis, 0, 0, tiled=False)
    return gathered.reshape((size * value.shape[0],) + value.shape[1:])


def sum_rows(value, axis):
    size = lax.axis_size(axis)
    parts = value.reshape((size, value.shape[0] // size) + value.shape[1:])
    received = lax.all_to_all(parts, axis, 0, 0, tiled=False)
    return jnp.sum(received.astype(jnp.float32), axis=0)


def split_three(value):
    high = value.astype(jnp.bfloat16)
    rest = value - high.astype(jnp.float32)
    middle = rest.astype(jnp.bfloat16)
    low = (rest - middle.astype(jnp.float32)).astype(jnp.bfloat16)
    return jnp.stack([high, middle, low])


def join_three(pieces):
    pieces = pieces.astype(jnp.float32)
    return pieces[..., 0] + pieces[..., 1] + pieces[..., 2]


def with_row(rows, pieces):
    extra = jnp.zeros((1, rows.shape[1]), rows.dtype).at[0, : pieces.shape[0]].set(pieces)
    return jnp.concatenate([rows, extra], axis=0)


def body(tokens, target, probe_vector, weight_in, weight_out, slot_rows, slot_count):
    columns, unit, slots, block, width_two = weight_in.shape
    features = tokens.shape[1]
    feature_blocks = features // block
    hidden_width = columns * block
    row_index = slot_rows[:, 0]
    in_use = lax.broadcasted_iota(jnp.int32, (columns, slots), 1) < slot_count[:, 0][:, None]
    mask_low = in_use.astype(jnp.bfloat16)[:, :, None, None]
    mask_full = in_use.astype(jnp.float32)[:, :, None, None]
    tiles_in = weight_in[:, 0] * mask_low
    tiles_out = weight_out[:, 0] * mask_low
    chosen = jnp.take(
        probe_vector.reshape(feature_blocks, block), row_index.reshape(-1), axis=0
    ).reshape(columns, slots, block)
    image_part = jnp.einsum(
        "jsk,jskn->jn", chosen, tiles_in.astype(jnp.float32), precision=lax.Precision.HIGHEST
    )
    x_full = gather_rows(tokens, "wide")
    image_and_norm = butterfly_sum(
        jnp.concatenate([image_part.reshape(-1), jnp.sum(probe_vector * probe_vector)[None]]), "blk"
    )
    x_full, image_and_norm = lax.optimization_barrier((x_full, image_and_norm))
    image = image_and_norm[:-1].reshape(image_part.shape)
    norm_probe = image_and_norm[-1]
    norm_image = butterfly_sum(jnp.sum(image * image)[None], "wide")[0]
    spectral = jnp.sqrt(norm_image / norm_probe)

    w1 = spread_tiles(tiles_in, row_index, feature_blocks).reshape(features, hidden_width)
    w2 = jnp.transpose(
        spread_tiles(tiles_out, row_index, feature_blocks), (2, 1, 0, 3)
    ).reshape(hidden_width, features)

    pre_part = jnp.dot(x_full, w1, preferred_element_type=jnp.float32)
    pre_own = lax.psum_scatter(
        pre_part.astype(jnp.bfloat16), "blk", scatter_dimension=0, tiled=True
    ).astype(jnp.float32)
    pre_own, spectral = lax.optimization_barrier((pre_own, spectral))
    hidden_own = pre_own / spectral
    active_own = activate(hidden_own).astype(jnp.bfloat16)
    active_full = lax.all_gather(active_own, "blk", axis=0, tiled=True)

    out_part = jnp.dot(active_full, w2, preferred_element_type=jnp.float32)
    outputs = sum_rows(out_part.astype(jnp.bfloat16), "wide").astype(jnp.bfloat16)
    residual = (outputs.astype(jnp.float32) - target.astype(jnp.float32)).astype(jnp.bfloat16)
    error_full = gather_rows(residual, "wide")

    back_part = lax.dot_general(
        error_full, w2, (((1,), (1,)), ((), ())), preferred_element_type=jnp.float32
    )
    back_own = lax.psum_scatter(
        back_part.astype(jnp.bfloat16), "blk", scatter_dimension=0, tiled=True
    ).astype(jnp.float32)
    slope_own = (back_own * activate_slope(hidden_own)).astype(jnp.bfloat16)
    curvature_part = jnp.sum(slope_own.astype(jnp.float32) * pre_own)
    slope_rows = lax.all_gather(
        with_row(slope_own, split_three(curvature_part)), "blk", axis=0, tiled=False
    )
    slope_full = slope_rows[:, :-1].reshape(-1, slope_own.shape[1])
    curvature_blk = jnp.sum(join_three(slope_rows[:, -1, :3]))

    in_part = lax.dot_general(
        slope_full, w1, (((1,), (1,)), ((), ())), preferred_element_type=jnp.float32
    )
    size = lax.axis_size("wide")
    in_rows = in_part.astype(jnp.bfloat16).reshape(size, -1, features)
    extra = jnp.zeros((size, 1, features), jnp.bfloat16).at[:, 0, :3].set(
        split_three(curvature_blk)[None]
    )
    received = lax.all_to_all(
        jnp.concatenate([in_rows, extra], axis=1), "wide", 0, 0, tiled=False
    )
    token_grad = (
        jnp.sum(received[:, :-1].astype(jnp.float32), axis=0) / spectral
    ).astype(jnp.bfloat16)
    curvature = jnp.sum(join_three(received[:, -1, :3]))

    g1 = lax.dot_general(
        x_full, slope_full, (((0,), (0,)), ((), ())), preferred_element_type=jnp.float32
    )
    raw_in = pick_tiles(g1.reshape(feature_blocks, block, columns, block), row_index) * mask_full
    g2 = lax.dot_general(
        error_full, active_full, (((0,), (0,)), ((), ())), preferred_element_type=jnp.float32
    )
    grad_out = pick_tiles(g2.reshape(feature_blocks, block, columns, block), row_index) * mask_full
    grad_out = jnp.transpose(grad_out, (0, 1, 3, 2))

    outer = jnp.einsum("jsk,jn->jskn", chosen, image) * mask_full
    grad_in = raw_in / spectral - curvature / (spectral**3 * norm_probe) * outer
    return (outputs, token_grad, grad_in[:, None], grad_out[:, None])


def solution(mesh):
    in_specs = (
        P("wide", "blk"),
        P("wide", "blk"),
        P("blk"),
        P("wide", "blk", None, None, None),
        P("wide", "blk", None, None, None),
        P("wide", "blk", None),
        P("wide", "blk"),
    )
    out_specs = (
        P("wide", "blk"),
        P("wide", "blk"),
        P("wide", "blk", None, None, None),
        P("wide", "blk", None, None, None),
    )
    return jax.shard_map(body, mesh=mesh, in_specs=in_specs, out_specs=out_specs, check_vma=False)
```

```python
import jax
import jax.numpy as jnp
from jax import lax
from jax.sharding import PartitionSpec as P


def activate(value):
    return jax.nn.gelu(value, approximate=True)


def activate_slope(value):
    return jax.jvp(activate, (value,), (jnp.ones_like(value),))[1]


def spread_tiles(tiles, row_index, feature_blocks):
    rows = lax.broadcasted_iota(jnp.int32, (feature_blocks,) + row_index.shape, 0)
    hit = rows == row_index[None]
    zero = jnp.zeros((), tiles.dtype)
    dense = jnp.where(hit[:, :, 0, None, None], tiles[None, :, 0], zero)
    for slot in range(1, row_index.shape[1]):
        dense = dense + jnp.where(hit[:, :, slot, None, None], tiles[None, :, slot], zero)
    return jnp.transpose(dense, (0, 2, 1, 3))


def pick_tiles(dense, row_index):
    feature_blocks = dense.shape[0]
    rows = lax.broadcasted_iota(jnp.int32, (feature_blocks,) + row_index.shape, 0)
    hit = rows == row_index[None]
    by_col = jnp.transpose(dense, (0, 2, 1, 3))
    picked = jnp.zeros(row_index.shape + dense.shape[1:2] + dense.shape[3:4], dense.dtype)
    for r in range(feature_blocks):
        picked = picked + jnp.where(hit[r][:, :, None, None], by_col[r][:, None], 0.0)
    return picked


def butterfly_sum(value, axis):
    size = lax.axis_size(axis)
    step = 1
    while step < size:
        value = value + lax.ppermute(value, axis, [(i, i ^ step) for i in range(size)])
        step *= 2
    return value


def gather_rows(value, axis):
    size = lax.axis_size(axis)
    spread = jnp.broadcast_to(value[None], (size,) + value.shape)
    gathered = lax.all_to_all(spread, axis, 0, 0, tiled=False)
    return gathered.reshape((size * value.shape[0],) + value.shape[1:])


def sum_rows(value, axis):
    size = lax.axis_size(axis)
    parts = value.reshape((size, value.shape[0] // size) + value.shape[1:])
    received = lax.all_to_all(parts, axis, 0, 0, tiled=False)
    return jnp.sum(received.astype(jnp.float32), axis=0)


def split_three(value):
    high = value.astype(jnp.bfloat16)
    rest = value - high.astype(jnp.float32)
    middle = rest.astype(jnp.bfloat16)
    low = (rest - middle.astype(jnp.float32)).astype(jnp.bfloat16)
    return jnp.stack([high, middle, low])


def join_three(pieces):
    pieces = pieces.astype(jnp.float32)
    return pieces[..., 0] + pieces[..., 1] + pieces[..., 2]


def with_row(rows, pieces):
    extra = jnp.zeros((1, rows.shape[1]), rows.dtype).at[0, : pieces.shape[0]].set(pieces)
    return jnp.concatenate([rows, extra], axis=0)


def body(tokens, target, probe_vector, weight_in, weight_out, slot_rows, slot_count):
    columns, unit, slots, block, width_two = weight_in.shape
    features = tokens.shape[1]
    feature_blocks = features // block
    hidden_width = columns * block
    row_index = slot_rows[:, 0]
    in_use = lax.broadcasted_iota(jnp.int32, (columns, slots), 1) < slot_count[:, 0][:, None]
    mask_low = in_use.astype(jnp.bfloat16)[:, :, None, None]
    mask_full = in_use.astype(jnp.float32)[:, :, None, None]
    tiles_in = weight_in[:, 0] * mask_low
    tiles_out = weight_out[:, 0] * mask_low
    chosen = jnp.take(
        probe_vector.reshape(feature_blocks, block), row_index.reshape(-1), axis=0
    ).reshape(columns, slots, block)
    image_part = jnp.einsum(
        "jsk,jskn->jn", chosen, tiles_in.astype(jnp.float32), precision=lax.Precision.HIGHEST
    )
    x_full = gather_rows(tokens, "wide")
    image_and_norm = butterfly_sum(
        jnp.concatenate([image_part.reshape(-1), jnp.sum(probe_vector * probe_vector)[None]]), "blk"
    )
    x_full, image_and_norm = lax.optimization_barrier((x_full, image_and_norm))
    image = image_and_norm[:-1].reshape(image_part.shape)
    norm_probe = image_and_norm[-1]
    norm_image = butterfly_sum(jnp.sum(image * image)[None], "wide")[0]
    spectral = jnp.sqrt(norm_image / norm_probe)

    w1 = spread_tiles(tiles_in, row_index, feature_blocks).reshape(features, hidden_width)
    w2 = jnp.transpose(
        spread_tiles(tiles_out, row_index, feature_blocks), (2, 1, 0, 3)
    ).reshape(hidden_width, features)

    pre_part = jnp.dot(x_full, w1, preferred_element_type=jnp.float32)
    pre_own = lax.psum_scatter(
        pre_part.astype(jnp.bfloat16), "blk", scatter_dimension=0, tiled=True
    ).astype(jnp.float32)
    pre_own, spectral = lax.optimization_barrier((pre_own, spectral))
    hidden_own = pre_own / spectral
    active_own = activate(hidden_own).astype(jnp.bfloat16)
    active_full = lax.all_gather(active_own, "blk", axis=0, tiled=True)

    out_part = jnp.dot(active_full, w2, preferred_element_type=jnp.float32)
    outputs = sum_rows(out_part.astype(jnp.bfloat16), "wide").astype(jnp.bfloat16)
    residual = (outputs.astype(jnp.float32) - target.astype(jnp.float32)).astype(jnp.bfloat16)
    error_full = gather_rows(residual, "wide")

    back_part = lax.dot_general(
        error_full, w2, (((1,), (1,)), ((), ())), preferred_element_type=jnp.float32
    )
    back_own = lax.psum_scatter(
        back_part.astype(jnp.bfloat16), "blk", scatter_dimension=0, tiled=True
    ).astype(jnp.float32)
    g2 = lax.dot_general(
        error_full, active_full, (((0,), (0,)), ((), ())), preferred_element_type=jnp.float32
    )
    grad_out = pick_tiles(g2.reshape(feature_blocks, block, columns, block), row_index) * mask_full
    grad_out = jnp.transpose(grad_out, (0, 1, 3, 2))
    back_own, grad_out = lax.optimization_barrier((back_own, grad_out))
    slope_own = (back_own * activate_slope(hidden_own)).astype(jnp.bfloat16)
    curvature_part = jnp.sum(slope_own.astype(jnp.float32) * pre_own)
    slope_rows = lax.all_gather(
        with_row(slope_own, split_three(curvature_part)), "blk", axis=0, tiled=False
    )
    slope_full = slope_rows[:, :-1].reshape(-1, slope_own.shape[1])
    curvature_blk = jnp.sum(join_three(slope_rows[:, -1, :3]))

    in_part = lax.dot_general(
        slope_full, w1, (((1,), (1,)), ((), ())), preferred_element_type=jnp.float32
    )
    size = lax.axis_size("wide")
    in_rows = in_part.astype(jnp.bfloat16).reshape(size, -1, features)
    extra = jnp.zeros((size, 1, features), jnp.bfloat16).at[:, 0, :3].set(
        split_three(curvature_blk)[None]
    )
    received = lax.all_to_all(
        jnp.concatenate([in_rows, extra], axis=1), "wide", 0, 0, tiled=False
    )
    token_grad = (
        jnp.sum(received[:, :-1].astype(jnp.float32), axis=0) / spectral
    ).astype(jnp.bfloat16)
    curvature = jnp.sum(join_three(received[:, -1, :3]))

    g1 = lax.dot_general(
        x_full, slope_full, (((0,), (0,)), ((), ())), preferred_element_type=jnp.float32
    )
    raw_in = pick_tiles(g1.reshape(feature_blocks, block, columns, block), row_index) * mask_full

    outer = jnp.einsum("jsk,jn->jskn", chosen, image) * mask_full
    grad_in = raw_in / spectral - curvature / (spectral**3 * norm_probe) * outer
    return (outputs, token_grad, grad_in[:, None], grad_out[:, None])


def solution(mesh):
    in_specs = (
        P("wide", "blk"),
        P("wide", "blk"),
        P("blk"),
        P("wide", "blk", None, None, None),
        P("wide", "blk", None, None, None),
        P("wide", "blk", None),
        P("wide", "blk"),
    )
    out_specs = (
        P("wide", "blk"),
        P("wide", "blk"),
        P("wide", "blk", None, None, None),
        P("wide", "blk", None, None, None),
    )
    return jax.shard_map(body, mesh=mesh, in_specs=in_specs, out_specs=out_specs, check_vma=False)
```

```python
import jax
import jax.numpy as jnp
from jax import lax
from jax.sharding import Mesh, PartitionSpec as P

WIDE = ("chip", "core")


def activate(value):
    return jax.nn.gelu(value, approximate=True)


def activate_slope(value):
    return jax.jvp(activate, (value,), (jnp.ones_like(value),))[1]


def spread_tiles(tiles, row_index, feature_blocks):
    rows = lax.broadcasted_iota(jnp.int32, (feature_blocks,) + row_index.shape, 0)
    hit = rows == row_index[None]
    zero = jnp.zeros((), tiles.dtype)
    dense = jnp.where(hit[:, :, 0, None, None], tiles[None, :, 0], zero)
    for slot in range(1, row_index.shape[1]):
        dense = dense + jnp.where(hit[:, :, slot, None, None], tiles[None, :, slot], zero)
    return jnp.transpose(dense, (0, 2, 1, 3))


def pick_tiles(dense, row_index):
    feature_blocks = dense.shape[0]
    rows = lax.broadcasted_iota(jnp.int32, (feature_blocks,) + row_index.shape, 0)
    hit = rows == row_index[None]
    by_col = jnp.transpose(dense, (0, 2, 1, 3))
    picked = jnp.zeros(row_index.shape + dense.shape[1:2] + dense.shape[3:4], dense.dtype)
    for r in range(feature_blocks):
        picked = picked + jnp.where(hit[r][:, :, None, None], by_col[r][:, None], 0.0)
    return picked


def group_size(axis):
    if isinstance(axis, tuple):
        size = 1
        for name in axis:
            size *= lax.axis_size(name)
        return size
    return lax.axis_size(axis)


def butterfly_sum(value, axis):
    size = group_size(axis)
    step = 1
    while step < size:
        value = value + lax.ppermute(value, axis, [(i, i ^ step) for i in range(size)])
        step *= 2
    return value


def gather_rows(value):
    chips = lax.axis_size("chip")
    spread = jnp.broadcast_to(value[None], (chips,) + value.shape)
    mine = lax.all_to_all(spread, "chip", 0, 0, tiled=False)
    other = lax.ppermute(mine, "core", [(0, 1), (1, 0)])
    first = lax.axis_index("core") == 0
    pair = jnp.where(first, jnp.stack([mine, other], 1), jnp.stack([other, mine], 1))
    return pair.reshape((-1,) + value.shape[1:])


def pair_rows(value):
    chips = lax.axis_size("chip")
    parts = value.reshape((chips, 2, -1) + value.shape[1:])
    first = lax.axis_index("core") == 0
    keep = jnp.where(first, parts[:, 0], parts[:, 1])
    give = jnp.where(first, parts[:, 1], parts[:, 0])
    got = lax.ppermute(give, "core", [(0, 1), (1, 0)])
    return (keep.astype(jnp.float32) + got.astype(jnp.float32)).astype(jnp.bfloat16)


def sum_rows(value):
    received = lax.all_to_all(pair_rows(value), "chip", 0, 0, tiled=False)
    return jnp.sum(received.astype(jnp.float32), axis=0)


def split_three(value):
    high = value.astype(jnp.bfloat16)
    rest = value - high.astype(jnp.float32)
    middle = rest.astype(jnp.bfloat16)
    low = (rest - middle.astype(jnp.float32)).astype(jnp.bfloat16)
    return jnp.stack([high, middle, low])


def join_three(pieces):
    pieces = pieces.astype(jnp.float32)
    return pieces[..., 0] + pieces[..., 1] + pieces[..., 2]


def with_row(rows, pieces):
    extra = jnp.zeros((1, rows.shape[1]), rows.dtype).at[0, : pieces.shape[0]].set(pieces)
    return jnp.concatenate([rows, extra], axis=0)


def body(tokens, target, probe_vector, weight_in, weight_out, slot_rows, slot_count):
    columns, unit, slots, block, width_two = weight_in.shape
    features = tokens.shape[1]
    feature_blocks = features // block
    hidden_width = columns * block
    row_index = slot_rows[:, 0]
    in_use = lax.broadcasted_iota(jnp.int32, (columns, slots), 1) < slot_count[:, 0][:, None]
    mask_low = in_use.astype(jnp.bfloat16)[:, :, None, None]
    mask_full = in_use.astype(jnp.float32)[:, :, None, None]
    tiles_in = weight_in[:, 0] * mask_low
    tiles_out = weight_out[:, 0] * mask_low
    chosen = jnp.take(
        probe_vector.reshape(feature_blocks, block), row_index.reshape(-1), axis=0
    ).reshape(columns, slots, block)
    image_part = jnp.einsum(
        "jsk,jskn->jn", chosen, tiles_in.astype(jnp.float32), precision=lax.Precision.HIGHEST
    )
    x_full = gather_rows(tokens)
    image_and_norm = butterfly_sum(
        jnp.concatenate([image_part.reshape(-1), jnp.sum(probe_vector * probe_vector)[None]]), "blk"
    )
    x_full, image_and_norm = lax.optimization_barrier((x_full, image_and_norm))
    image = image_and_norm[:-1].reshape(image_part.shape)
    norm_probe = image_and_norm[-1]
    norm_image = butterfly_sum(jnp.sum(image * image)[None], WIDE)[0]
    spectral = jnp.sqrt(norm_image / norm_probe)

    w1 = spread_tiles(tiles_in, row_index, feature_blocks).reshape(features, hidden_width)
    w2 = jnp.transpose(
        spread_tiles(tiles_out, row_index, feature_blocks), (2, 1, 0, 3)
    ).reshape(hidden_width, features)

    pre_part = jnp.dot(x_full, w1, preferred_element_type=jnp.float32)
    pre_own = lax.psum_scatter(
        pre_part.astype(jnp.bfloat16), "blk", scatter_dimension=0, tiled=True
    ).astype(jnp.float32)
    pre_own, spectral = lax.optimization_barrier((pre_own, spectral))
    hidden_own = pre_own / spectral
    active_own = activate(hidden_own).astype(jnp.bfloat16)
    active_full = lax.all_gather(active_own, "blk", axis=0, tiled=True)

    out_part = jnp.dot(active_full, w2, preferred_element_type=jnp.float32)
    outputs = sum_rows(out_part.astype(jnp.bfloat16)).astype(jnp.bfloat16)
    residual = (outputs.astype(jnp.float32) - target.astype(jnp.float32)).astype(jnp.bfloat16)
    error_full = gather_rows(residual)

    back_part = lax.dot_general(
        error_full, w2, (((1,), (1,)), ((), ())), preferred_element_type=jnp.float32
    )
    back_own = lax.psum_scatter(
        back_part.astype(jnp.bfloat16), "blk", scatter_dimension=0, tiled=True
    ).astype(jnp.float32)
    g2 = lax.dot_general(
        error_full, active_full, (((0,), (0,)), ((), ())), preferred_element_type=jnp.float32
    )
    grad_out = pick_tiles(g2.reshape(feature_blocks, block, columns, block), row_index) * mask_full
    grad_out = jnp.transpose(grad_out, (0, 1, 3, 2))
    back_own, grad_out = lax.optimization_barrier((back_own, grad_out))
    slope_own = (back_own * activate_slope(hidden_own)).astype(jnp.bfloat16)
    curvature_part = jnp.sum(slope_own.astype(jnp.float32) * pre_own)
    slope_rows = lax.all_gather(
        with_row(slope_own, split_three(curvature_part)), "blk", axis=0, tiled=False
    )
    slope_full = slope_rows[:, :-1].reshape(-1, slope_own.shape[1])
    curvature_blk = jnp.sum(join_three(slope_rows[:, -1, :3]))

    in_part = lax.dot_general(
        slope_full, w1, (((1,), (1,)), ((), ())), preferred_element_type=jnp.float32
    )
    in_rows = pair_rows(in_part.astype(jnp.bfloat16))
    curvature_chip = curvature_blk + lax.ppermute(curvature_blk, "core", [(0, 1), (1, 0)])
    extra = jnp.zeros((in_rows.shape[0], 1, features), jnp.bfloat16).at[:, 0, :3].set(
        split_three(curvature_chip)[None]
    )
    received = lax.all_to_all(
        jnp.concatenate([in_rows, extra], axis=1), "chip", 0, 0, tiled=False
    )
    token_grad = (
        jnp.sum(received[:, :-1].astype(jnp.float32), axis=0) / spectral
    ).astype(jnp.bfloat16)
    curvature = jnp.sum(join_three(received[:, -1, :3]))

    g1 = lax.dot_general(
        x_full, slope_full, (((0,), (0,)), ((), ())), preferred_element_type=jnp.float32
    )
    raw_in = pick_tiles(g1.reshape(feature_blocks, block, columns, block), row_index) * mask_full

    outer = jnp.einsum("jsk,jn->jskn", chosen, image) * mask_full
    grad_in = raw_in / spectral - curvature / (spectral**3 * norm_probe) * outer
    return (outputs, token_grad, grad_in[:, None], grad_out[:, None])


def solution(mesh):
    wide, blk = mesh.shape["wide"], mesh.shape["blk"]
    split = Mesh(mesh.devices.reshape(wide // 2, 2, blk), ("chip", "core", "blk"))
    in_specs = (
        P(WIDE, "blk"),
        P(WIDE, "blk"),
        P("blk"),
        P(WIDE, "blk", None, None, None),
        P(WIDE, "blk", None, None, None),
        P(WIDE, "blk", None),
        P(WIDE, "blk"),
    )
    out_specs = (
        P(WIDE, "blk"),
        P(WIDE, "blk"),
        P(WIDE, "blk", None, None, None),
        P(WIDE, "blk", None, None, None),
    )
    return jax.shard_map(body, mesh=split, in_specs=in_specs, out_specs=out_specs, check_vma=False)
```

```python
import jax
import jax.numpy as jnp
from jax import lax
from jax.sharding import Mesh, PartitionSpec as P

WIDE = ("chip", "core")


def activate(value):
    return jax.nn.gelu(value, approximate=True)


def activate_slope(value):
    return jax.jvp(activate, (value,), (jnp.ones_like(value),))[1]


def spread_tiles(tiles, row_index, feature_blocks):
    rows = lax.broadcasted_iota(jnp.int32, (feature_blocks,) + row_index.shape, 0)
    hit = rows == row_index[None]
    zero = jnp.zeros((), tiles.dtype)
    dense = jnp.where(hit[:, :, 0, None, None], tiles[None, :, 0], zero)
    for slot in range(1, row_index.shape[1]):
        dense = dense + jnp.where(hit[:, :, slot, None, None], tiles[None, :, slot], zero)
    return jnp.transpose(dense, (0, 2, 1, 3))


def pick_tiles(dense, row_index):
    feature_blocks = dense.shape[0]
    rows = lax.broadcasted_iota(jnp.int32, (feature_blocks,) + row_index.shape, 0)
    hit = rows == row_index[None]
    by_col = jnp.transpose(dense, (0, 2, 1, 3))
    picked = jnp.zeros(row_index.shape + dense.shape[1:2] + dense.shape[3:4], dense.dtype)
    for r in range(feature_blocks):
        picked = picked + jnp.where(hit[r][:, :, None, None], by_col[r][:, None], 0.0)
    return picked


def group_size(axis):
    if isinstance(axis, tuple):
        size = 1
        for name in axis:
            size *= lax.axis_size(name)
        return size
    return lax.axis_size(axis)


def butterfly_sum(value, axis):
    size = group_size(axis)
    step = 1
    while step < size:
        value = value + lax.ppermute(value, axis, [(i, i ^ step) for i in range(size)])
        step *= 2
    return value


def gather_rows(value):
    chips = lax.axis_size("chip")
    spread = jnp.broadcast_to(value[None], (chips,) + value.shape)
    mine = lax.all_to_all(spread, "chip", 0, 0, tiled=False)
    other = lax.ppermute(mine, "core", [(0, 1), (1, 0)])
    first = lax.axis_index("core") == 0
    pair = jnp.where(first, jnp.stack([mine, other], 1), jnp.stack([other, mine], 1))
    return pair.reshape((-1,) + value.shape[1:])


def pair_rows(value):
    chips = lax.axis_size("chip")
    parts = value.reshape((chips, 2, -1) + value.shape[1:])
    first = lax.axis_index("core") == 0
    keep = jnp.where(first, parts[:, 0], parts[:, 1])
    give = jnp.where(first, parts[:, 1], parts[:, 0])
    got = lax.ppermute(give, "core", [(0, 1), (1, 0)])
    return (keep.astype(jnp.float32) + got.astype(jnp.float32)).astype(jnp.bfloat16)


def sum_rows(value):
    received = lax.all_to_all(pair_rows(value), "chip", 0, 0, tiled=False)
    return jnp.sum(received.astype(jnp.float32), axis=0)


def split_three(value):
    high = value.astype(jnp.bfloat16)
    rest = value - high.astype(jnp.float32)
    middle = rest.astype(jnp.bfloat16)
    low = (rest - middle.astype(jnp.float32)).astype(jnp.bfloat16)
    return jnp.stack([high, middle, low])


def join_three(pieces):
    pieces = pieces.astype(jnp.float32)
    return pieces[..., 0] + pieces[..., 1] + pieces[..., 2]


def with_row(rows, pieces):
    extra = jnp.zeros((1, rows.shape[1]), rows.dtype).at[0, : pieces.shape[0]].set(pieces)
    return jnp.concatenate([rows, extra], axis=0)


def body(tokens, target, probe_vector, weight_in, weight_out, slot_rows, slot_count):
    columns, unit, slots, block, width_two = weight_in.shape
    features = tokens.shape[1]
    feature_blocks = features // block
    hidden_width = columns * block
    row_index = slot_rows[:, 0]
    in_use = lax.broadcasted_iota(jnp.int32, (columns, slots), 1) < slot_count[:, 0][:, None]
    mask_low = in_use.astype(jnp.bfloat16)[:, :, None, None]
    mask_full = in_use.astype(jnp.float32)[:, :, None, None]
    tiles_in = weight_in[:, 0] * mask_low
    tiles_out = weight_out[:, 0] * mask_low
    chosen = jnp.take(
        probe_vector.reshape(feature_blocks, block), row_index.reshape(-1), axis=0
    ).reshape(columns, slots, block)
    image_part = jnp.einsum(
        "jsk,jskn->jn", chosen, tiles_in.astype(jnp.float32), precision=lax.Precision.HIGHEST
    )
    chunks = 2
    chunk_rows = tokens.shape[0] // chunks
    x_parts = [
        gather_rows(tokens[chunk * chunk_rows : (chunk + 1) * chunk_rows]) for chunk in range(chunks)
    ]
    image_and_norm = butterfly_sum(
        jnp.concatenate([image_part.reshape(-1), jnp.sum(probe_vector * probe_vector)[None]]), "blk"
    )
    x_parts[0], image_and_norm = lax.optimization_barrier((x_parts[0], image_and_norm))
    image = image_and_norm[:-1].reshape(image_part.shape)
    norm_probe = image_and_norm[-1]
    norm_image = butterfly_sum(jnp.sum(image * image)[None], WIDE)[0]
    spectral = jnp.sqrt(norm_image / norm_probe)

    w1 = spread_tiles(tiles_in, row_index, feature_blocks).reshape(features, hidden_width)
    w2 = jnp.transpose(
        spread_tiles(tiles_out, row_index, feature_blocks), (2, 1, 0, 3)
    ).reshape(hidden_width, features)

    def blk_sum(part):
        return lax.psum_scatter(
            part.astype(jnp.bfloat16), "blk", scatter_dimension=0, tiled=True
        ).astype(jnp.float32)

    def by_rows(left, right):
        return lax.dot_general(left, right, (((1,), (1,)), ((), ())), preferred_element_type=jnp.float32)

    def by_tokens(left, right):
        return lax.dot_general(left, right, (((0,), (0,)), ((), ())), preferred_element_type=jnp.float32)

    pre_own = [blk_sum(jnp.dot(x, w1, preferred_element_type=jnp.float32)) for x in x_parts]
    pre_own[0], spectral = lax.optimization_barrier((pre_own[0], spectral))
    hidden_own = [pre / spectral for pre in pre_own]
    active_full = [
        lax.all_gather(activate(hidden).astype(jnp.bfloat16), "blk", axis=0, tiled=True)
        for hidden in hidden_own
    ]
    outputs = []
    error_full = []
    for chunk, active in enumerate(active_full):
        out_part = jnp.dot(active, w2, preferred_element_type=jnp.float32)
        outputs.append(sum_rows(out_part.astype(jnp.bfloat16)).astype(jnp.bfloat16))
        target_part = target[chunk * chunk_rows : (chunk + 1) * chunk_rows]
        residual = (outputs[-1].astype(jnp.float32) - target_part.astype(jnp.float32)).astype(
            jnp.bfloat16
        )
        error_full.append(gather_rows(residual))
    back_own = [blk_sum(by_rows(error, w2)) for error in error_full]
    g2 = by_tokens(error_full[0], active_full[0])
    for error, active in zip(error_full[1:], active_full[1:]):
        g2 = g2 + by_tokens(error, active)
    grad_out = pick_tiles(g2.reshape(feature_blocks, block, columns, block), row_index) * mask_full
    grad_out = jnp.transpose(grad_out, (0, 1, 3, 2))
    back_own[-1], grad_out = lax.optimization_barrier((back_own[-1], grad_out))
    slope_own = [
        (back * activate_slope(hidden)).astype(jnp.bfloat16)
        for back, hidden in zip(back_own, hidden_own)
    ]
    curvature_part = jnp.sum(slope_own[0].astype(jnp.float32) * pre_own[0])
    for slope, pre in zip(slope_own[1:], pre_own[1:]):
        curvature_part = curvature_part + jnp.sum(slope.astype(jnp.float32) * pre)
    slope_full = [lax.all_gather(slope, "blk", axis=0, tiled=True) for slope in slope_own[:-1]]
    slope_rows = lax.all_gather(
        with_row(slope_own[-1], split_three(curvature_part)), "blk", axis=0, tiled=False
    )
    slope_full.append(slope_rows[:, :-1].reshape(-1, slope_own[-1].shape[1]))
    curvature_blk = jnp.sum(join_three(slope_rows[:, -1, :3]))

    token_grad = [
        (sum_rows(by_rows(slope, w1).astype(jnp.bfloat16)) / spectral).astype(jnp.bfloat16)
        for slope in slope_full[:-1]
    ]
    in_rows = pair_rows(by_rows(slope_full[-1], w1).astype(jnp.bfloat16))
    curvature_chip = curvature_blk + lax.ppermute(curvature_blk, "core", [(0, 1), (1, 0)])
    extra = jnp.zeros((in_rows.shape[0], 1, features), jnp.bfloat16).at[:, 0, :3].set(
        split_three(curvature_chip)[None]
    )
    received = lax.all_to_all(
        jnp.concatenate([in_rows, extra], axis=1), "chip", 0, 0, tiled=False
    )
    token_grad.append(
        (jnp.sum(received[:, :-1].astype(jnp.float32), axis=0) / spectral).astype(jnp.bfloat16)
    )
    curvature = jnp.sum(join_three(received[:, -1, :3]))

    g1 = by_tokens(x_parts[0], slope_full[0])
    for x, slope in zip(x_parts[1:], slope_full[1:]):
        g1 = g1 + by_tokens(x, slope)
    raw_in = pick_tiles(g1.reshape(feature_blocks, block, columns, block), row_index) * mask_full
    outputs = jnp.concatenate(outputs, axis=0)
    token_grad = jnp.concatenate(token_grad, axis=0)

    outer = jnp.einsum("jsk,jn->jskn", chosen, image) * mask_full
    grad_in = raw_in / spectral - curvature / (spectral**3 * norm_probe) * outer
    return (outputs, token_grad, grad_in[:, None], grad_out[:, None])


def solution(mesh):
    wide, blk = mesh.shape["wide"], mesh.shape["blk"]
    split = Mesh(mesh.devices.reshape(wide // 2, 2, blk), ("chip", "core", "blk"))
    in_specs = (
        P(WIDE, "blk"),
        P(WIDE, "blk"),
        P("blk"),
        P(WIDE, "blk", None, None, None),
        P(WIDE, "blk", None, None, None),
        P(WIDE, "blk", None),
        P(WIDE, "blk"),
    )
    out_specs = (
        P(WIDE, "blk"),
        P(WIDE, "blk"),
        P(WIDE, "blk", None, None, None),
        P(WIDE, "blk", None, None, None),
    )
    return jax.shard_map(body, mesh=split, in_specs=in_specs, out_specs=out_specs, check_vma=False)
```

```python
import jax
import jax.numpy as jnp
from jax import lax
from jax.sharding import Mesh, PartitionSpec as P

WIDE = ("chip", "core")


def activate(value):
    return jax.nn.gelu(value, approximate=True)


def activate_slope(value):
    return jax.jvp(activate, (value,), (jnp.ones_like(value),))[1]


def spread_tiles(tiles, row_index, feature_blocks):
    rows = lax.broadcasted_iota(jnp.int32, (feature_blocks,) + row_index.shape, 0)
    hit = rows == row_index[None]
    zero = jnp.zeros((), tiles.dtype)
    dense = jnp.where(hit[:, :, 0, None, None], tiles[None, :, 0], zero)
    for slot in range(1, row_index.shape[1]):
        dense = dense + jnp.where(hit[:, :, slot, None, None], tiles[None, :, slot], zero)
    return jnp.transpose(dense, (0, 2, 1, 3))


def pick_tiles(dense, row_index):
    feature_blocks = dense.shape[0]
    rows = lax.broadcasted_iota(jnp.int32, (feature_blocks,) + row_index.shape, 0)
    hit = rows == row_index[None]
    by_col = jnp.transpose(dense, (0, 2, 1, 3))
    picked = jnp.zeros(row_index.shape + dense.shape[1:2] + dense.shape[3:4], dense.dtype)
    for r in range(feature_blocks):
        picked = picked + jnp.where(hit[r][:, :, None, None], by_col[r][:, None], 0.0)
    return picked


def group_size(axis):
    if isinstance(axis, tuple):
        size = 1
        for name in axis:
            size *= lax.axis_size(name)
        return size
    return lax.axis_size(axis)


def butterfly_sum(value, axis):
    size = group_size(axis)
    step = 1
    while step < size:
        value = value + lax.ppermute(value, axis, [(i, i ^ step) for i in range(size)])
        step *= 2
    return value


def gather_rows(value):
    chips = lax.axis_size("chip")
    spread = jnp.broadcast_to(value[None], (chips,) + value.shape)
    mine = lax.all_to_all(spread, "chip", 0, 0, tiled=False)
    other = lax.ppermute(mine, "core", [(0, 1), (1, 0)])
    first = lax.axis_index("core") == 0
    pair = jnp.where(first, jnp.stack([mine, other], 1), jnp.stack([other, mine], 1))
    return pair.reshape((-1,) + value.shape[1:])


def pair_rows(value):
    chips = lax.axis_size("chip")
    parts = value.reshape((chips, 2, -1) + value.shape[1:])
    first = lax.axis_index("core") == 0
    keep = jnp.where(first, parts[:, 0], parts[:, 1])
    give = jnp.where(first, parts[:, 1], parts[:, 0])
    got = lax.ppermute(give, "core", [(0, 1), (1, 0)])
    return (keep.astype(jnp.float32) + got.astype(jnp.float32)).astype(jnp.bfloat16)


def sum_rows(value):
    received = lax.all_to_all(pair_rows(value), "chip", 0, 0, tiled=False)
    return jnp.sum(received.astype(jnp.float32), axis=0)


def split_three(value):
    high = value.astype(jnp.bfloat16)
    rest = value - high.astype(jnp.float32)
    middle = rest.astype(jnp.bfloat16)
    low = (rest - middle.astype(jnp.float32)).astype(jnp.bfloat16)
    return jnp.stack([high, middle, low])


def join_three(pieces):
    pieces = pieces.astype(jnp.float32)
    return pieces[..., 0] + pieces[..., 1] + pieces[..., 2]


def with_row(rows, pieces):
    extra = jnp.zeros((1, rows.shape[1]), rows.dtype).at[0, : pieces.shape[0]].set(pieces)
    return jnp.concatenate([rows, extra], axis=0)


def body(tokens, target, probe_vector, weight_in, weight_out, slot_rows, slot_count):
    columns, unit, slots, block, width_two = weight_in.shape
    features = tokens.shape[1]
    feature_blocks = features // block
    hidden_width = columns * block
    row_index = slot_rows[:, 0]
    in_use = lax.broadcasted_iota(jnp.int32, (columns, slots), 1) < slot_count[:, 0][:, None]
    mask_low = in_use.astype(jnp.bfloat16)[:, :, None, None]
    mask_full = in_use.astype(jnp.float32)[:, :, None, None]
    tiles_in = weight_in[:, 0] * mask_low
    tiles_out = weight_out[:, 0] * mask_low
    chosen = jnp.take(
        probe_vector.reshape(feature_blocks, block), row_index.reshape(-1), axis=0
    ).reshape(columns, slots, block)
    image_part = jnp.einsum(
        "jsk,jskn->jn", chosen, tiles_in.astype(jnp.float32), precision=lax.Precision.HIGHEST
    )
    x_full = gather_rows(tokens)
    image_and_norm = butterfly_sum(
        jnp.concatenate([image_part.reshape(-1), jnp.sum(probe_vector * probe_vector)[None]]), "blk"
    )
    x_full, image_and_norm = lax.optimization_barrier((x_full, image_and_norm))
    image = image_and_norm[:-1].reshape(image_part.shape)
    norm_probe = image_and_norm[-1]
    norm_image = butterfly_sum(jnp.sum(image * image)[None], WIDE)[0]
    spectral = jnp.sqrt(norm_image / norm_probe)

    w1 = spread_tiles(tiles_in, row_index, feature_blocks).reshape(features, hidden_width)
    w2 = jnp.transpose(
        spread_tiles(tiles_out, row_index, feature_blocks), (2, 1, 0, 3)
    ).reshape(hidden_width, features)

    pre_part = jnp.dot(x_full, w1, preferred_element_type=jnp.float32)
    pre_full = lax.psum(pre_part.astype(jnp.bfloat16), "blk").astype(jnp.float32)
    pre_full, spectral = lax.optimization_barrier((pre_full, spectral))
    hidden_full = pre_full / spectral
    active_full = activate(hidden_full).astype(jnp.bfloat16)

    out_part = jnp.dot(active_full, w2, preferred_element_type=jnp.float32)
    outputs = sum_rows(out_part.astype(jnp.bfloat16)).astype(jnp.bfloat16)
    residual = (outputs.astype(jnp.float32) - target.astype(jnp.float32)).astype(jnp.bfloat16)
    error_full = gather_rows(residual)

    back_part = lax.dot_general(
        error_full, w2, (((1,), (1,)), ((), ())), preferred_element_type=jnp.float32
    )
    back_full = lax.psum(back_part.astype(jnp.bfloat16), "blk").astype(jnp.float32)
    g2 = lax.dot_general(
        error_full, active_full, (((0,), (0,)), ((), ())), preferred_element_type=jnp.float32
    )
    grad_out = pick_tiles(g2.reshape(feature_blocks, block, columns, block), row_index) * mask_full
    grad_out = jnp.transpose(grad_out, (0, 1, 3, 2))
    back_full, grad_out = lax.optimization_barrier((back_full, grad_out))
    slope_full = (back_full * activate_slope(hidden_full)).astype(jnp.bfloat16)
    curvature_blk = jnp.sum(slope_full.astype(jnp.float32) * pre_full)

    in_part = lax.dot_general(
        slope_full, w1, (((1,), (1,)), ((), ())), preferred_element_type=jnp.float32
    )
    in_rows = pair_rows(in_part.astype(jnp.bfloat16))
    curvature_chip = curvature_blk + lax.ppermute(curvature_blk, "core", [(0, 1), (1, 0)])
    extra = jnp.zeros((in_rows.shape[0], 1, features), jnp.bfloat16).at[:, 0, :3].set(
        split_three(curvature_chip)[None]
    )
    received = lax.all_to_all(
        jnp.concatenate([in_rows, extra], axis=1), "chip", 0, 0, tiled=False
    )
    token_grad = (
        jnp.sum(received[:, :-1].astype(jnp.float32), axis=0) / spectral
    ).astype(jnp.bfloat16)
    curvature = jnp.sum(join_three(received[:, -1, :3]))

    g1 = lax.dot_general(
        x_full, slope_full, (((0,), (0,)), ((), ())), preferred_element_type=jnp.float32
    )
    raw_in = pick_tiles(g1.reshape(feature_blocks, block, columns, block), row_index) * mask_full

    outer = jnp.einsum("jsk,jn->jskn", chosen, image) * mask_full
    grad_in = raw_in / spectral - curvature / (spectral**3 * norm_probe) * outer
    return (outputs, token_grad, grad_in[:, None], grad_out[:, None])


def solution(mesh):
    wide, blk = mesh.shape["wide"], mesh.shape["blk"]
    split = Mesh(mesh.devices.reshape(wide // 2, 2, blk), ("chip", "core", "blk"))
    in_specs = (
        P(WIDE, "blk"),
        P(WIDE, "blk"),
        P("blk"),
        P(WIDE, "blk", None, None, None),
        P(WIDE, "blk", None, None, None),
        P(WIDE, "blk", None),
        P(WIDE, "blk"),
    )
    out_specs = (
        P(WIDE, "blk"),
        P(WIDE, "blk"),
        P(WIDE, "blk", None, None, None),
        P(WIDE, "blk", None, None, None),
    )
    return jax.shard_map(body, mesh=split, in_specs=in_specs, out_specs=out_specs, check_vma=False)
```

```python
import jax
import jax.numpy as jnp
from jax import lax
from jax.sharding import Mesh, PartitionSpec as P

WIDE = ("chip", "core")


def activate(value):
    return jax.nn.gelu(value, approximate=True)


def activate_slope(value):
    return jax.jvp(activate, (value,), (jnp.ones_like(value),))[1]


def spread_tiles(tiles, row_index, feature_blocks):
    rows = lax.broadcasted_iota(jnp.int32, (feature_blocks,) + row_index.shape, 0)
    hit = rows == row_index[None]
    zero = jnp.zeros((), tiles.dtype)
    dense = jnp.where(hit[:, :, 0, None, None], tiles[None, :, 0], zero)
    for slot in range(1, row_index.shape[1]):
        dense = dense + jnp.where(hit[:, :, slot, None, None], tiles[None, :, slot], zero)
    return jnp.transpose(dense, (0, 2, 1, 3))


def pick_tiles(dense, row_index):
    feature_blocks = dense.shape[0]
    rows = lax.broadcasted_iota(jnp.int32, (feature_blocks,) + row_index.shape, 0)
    hit = rows == row_index[None]
    by_col = jnp.transpose(dense, (0, 2, 1, 3))
    picked = jnp.zeros(row_index.shape + dense.shape[1:2] + dense.shape[3:4], dense.dtype)
    for r in range(feature_blocks):
        picked = picked + jnp.where(hit[r][:, :, None, None], by_col[r][:, None], 0.0)
    return picked


def group_size(axis):
    if isinstance(axis, tuple):
        size = 1
        for name in axis:
            size *= lax.axis_size(name)
        return size
    return lax.axis_size(axis)


def butterfly_sum(value, axis):
    size = group_size(axis)
    step = 1
    while step < size:
        value = value + lax.ppermute(value, axis, [(i, i ^ step) for i in range(size)])
        step *= 2
    return value


def gather_rows(value):
    chips = lax.axis_size("chip")
    spread = jnp.broadcast_to(value[None], (chips,) + value.shape)
    mine = lax.all_to_all(spread, "chip", 0, 0, tiled=False)
    other = lax.ppermute(mine, "core", [(0, 1), (1, 0)])
    first = lax.axis_index("core") == 0
    pair = jnp.where(first, jnp.stack([mine, other], 1), jnp.stack([other, mine], 1))
    return pair.reshape((-1,) + value.shape[1:])


def pair_rows(value):
    chips = lax.axis_size("chip")
    parts = value.reshape((chips, 2, -1) + value.shape[1:])
    first = lax.axis_index("core") == 0
    keep = jnp.where(first, parts[:, 0], parts[:, 1])
    give = jnp.where(first, parts[:, 1], parts[:, 0])
    got = lax.ppermute(give, "core", [(0, 1), (1, 0)])
    return (keep.astype(jnp.float32) + got.astype(jnp.float32)).astype(jnp.bfloat16)


def sum_rows(value):
    received = lax.all_to_all(pair_rows(value), "chip", 0, 0, tiled=False)
    return jnp.sum(received.astype(jnp.float32), axis=0)


def split_three(value):
    high = value.astype(jnp.bfloat16)
    rest = value - high.astype(jnp.float32)
    middle = rest.astype(jnp.bfloat16)
    low = (rest - middle.astype(jnp.float32)).astype(jnp.bfloat16)
    return jnp.stack([high, middle, low])


def join_three(pieces):
    pieces = pieces.astype(jnp.float32)
    return pieces[..., 0] + pieces[..., 1] + pieces[..., 2]


def with_row(rows, pieces):
    extra = jnp.zeros((1, rows.shape[1]), rows.dtype).at[0, : pieces.shape[0]].set(pieces)
    return jnp.concatenate([rows, extra], axis=0)


def body(tokens, target, probe_vector, weight_in, weight_out, slot_rows, slot_count):
    columns, unit, slots, block, width_two = weight_in.shape
    features = tokens.shape[1]
    feature_blocks = features // block
    hidden_width = columns * block
    row_index = slot_rows[:, 0]
    in_use = lax.broadcasted_iota(jnp.int32, (columns, slots), 1) < slot_count[:, 0][:, None]
    mask_low = in_use.astype(jnp.bfloat16)[:, :, None, None]
    mask_full = in_use.astype(jnp.float32)[:, :, None, None]
    tiles_in = weight_in[:, 0] * mask_low
    tiles_out = weight_out[:, 0] * mask_low
    chosen = jnp.take(
        probe_vector.reshape(feature_blocks, block), row_index.reshape(-1), axis=0
    ).reshape(columns, slots, block)
    image_part = jnp.einsum(
        "jsk,jskn->jn", chosen, tiles_in.astype(jnp.float32), precision=lax.Precision.HIGHEST
    )
    x_full = gather_rows(tokens)
    image_and_norm = butterfly_sum(
        jnp.concatenate([image_part.reshape(-1), jnp.sum(probe_vector * probe_vector)[None]]), "blk"
    )
    image = image_and_norm[:-1].reshape(image_part.shape)
    norm_probe = image_and_norm[-1]
    norm_image = butterfly_sum(jnp.sum(image * image)[None], WIDE)[0]
    spectral = jnp.sqrt(norm_image / norm_probe)

    w1 = spread_tiles(tiles_in, row_index, feature_blocks).reshape(features, hidden_width)
    w2 = jnp.transpose(
        spread_tiles(tiles_out, row_index, feature_blocks), (2, 1, 0, 3)
    ).reshape(hidden_width, features)

    pre_part = jnp.dot(x_full, w1, preferred_element_type=jnp.float32)
    pre_own = lax.psum_scatter(
        pre_part.astype(jnp.bfloat16), "blk", scatter_dimension=0, tiled=True
    ).astype(jnp.float32)
    pre_own, spectral = lax.optimization_barrier((pre_own, spectral))
    hidden_own = pre_own / spectral
    active_own = activate(hidden_own).astype(jnp.bfloat16)
    active_full = lax.all_gather(active_own, "blk", axis=0, tiled=True)

    out_part = jnp.dot(active_full, w2, preferred_element_type=jnp.float32)
    outputs = sum_rows(out_part.astype(jnp.bfloat16)).astype(jnp.bfloat16)
    residual = (outputs.astype(jnp.float32) - target.astype(jnp.float32)).astype(jnp.bfloat16)
    error_full = gather_rows(residual)

    back_part = lax.dot_general(
        error_full, w2, (((1,), (1,)), ((), ())), preferred_element_type=jnp.float32
    )
    back_own = lax.psum_scatter(
        back_part.astype(jnp.bfloat16), "blk", scatter_dimension=0, tiled=True
    ).astype(jnp.float32)
    g2 = lax.dot_general(
        error_full, active_full, (((0,), (0,)), ((), ())), preferred_element_type=jnp.float32
    )
    grad_out = pick_tiles(g2.reshape(feature_blocks, block, columns, block), row_index) * mask_full
    grad_out = jnp.transpose(grad_out, (0, 1, 3, 2))
    back_own, grad_out = lax.optimization_barrier((back_own, grad_out))
    slope_own = (back_own * activate_slope(hidden_own)).astype(jnp.bfloat16)
    curvature_part = jnp.sum(slope_own.astype(jnp.float32) * pre_own)
    slope_rows = lax.all_gather(
        with_row(slope_own, split_three(curvature_part)), "blk", axis=0, tiled=False
    )
    slope_full = slope_rows[:, :-1].reshape(-1, slope_own.shape[1])
    curvature_blk = jnp.sum(join_three(slope_rows[:, -1, :3]))

    in_part = lax.dot_general(
        slope_full, w1, (((1,), (1,)), ((), ())), preferred_element_type=jnp.float32
    )
    in_rows = pair_rows(in_part.astype(jnp.bfloat16))
    curvature_chip = curvature_blk + lax.ppermute(curvature_blk, "core", [(0, 1), (1, 0)])
    extra = jnp.zeros((in_rows.shape[0], 1, features), jnp.bfloat16).at[:, 0, :3].set(
        split_three(curvature_chip)[None]
    )
    received = lax.all_to_all(
        jnp.concatenate([in_rows, extra], axis=1), "chip", 0, 0, tiled=False
    )
    token_grad = (
        jnp.sum(received[:, :-1].astype(jnp.float32), axis=0) / spectral
    ).astype(jnp.bfloat16)
    curvature = jnp.sum(join_three(received[:, -1, :3]))

    g1 = lax.dot_general(
        x_full, slope_full, (((0,), (0,)), ((), ())), preferred_element_type=jnp.float32
    )
    raw_in = pick_tiles(g1.reshape(feature_blocks, block, columns, block), row_index) * mask_full

    outer = jnp.einsum("jsk,jn->jskn", chosen, image) * mask_full
    grad_in = raw_in / spectral - curvature / (spectral**3 * norm_probe) * outer
    return (outputs, token_grad, grad_in[:, None], grad_out[:, None])


def solution(mesh):
    wide, blk = mesh.shape["wide"], mesh.shape["blk"]
    split = Mesh(mesh.devices.reshape(wide // 2, 2, blk), ("chip", "core", "blk"))
    in_specs = (
        P(WIDE, "blk"),
        P(WIDE, "blk"),
        P("blk"),
        P(WIDE, "blk", None, None, None),
        P(WIDE, "blk", None, None, None),
        P(WIDE, "blk", None),
        P(WIDE, "blk"),
    )
    out_specs = (
        P(WIDE, "blk"),
        P(WIDE, "blk"),
        P(WIDE, "blk", None, None, None),
        P(WIDE, "blk", None, None, None),
    )
    return jax.shard_map(body, mesh=split, in_specs=in_specs, out_specs=out_specs, check_vma=False)
```

```python
import jax
import jax.numpy as jnp
from jax import lax
from jax.sharding import Mesh, PartitionSpec as P

WIDE = ("chip", "core")


def activate(value):
    return jax.nn.gelu(value, approximate=True)


def activate_slope(value):
    return jax.jvp(activate, (value,), (jnp.ones_like(value),))[1]


def spread_tiles(tiles, row_index, feature_blocks):
    rows = lax.broadcasted_iota(jnp.int32, (feature_blocks,) + row_index.shape, 0)
    hit = rows == row_index[None]
    zero = jnp.zeros((), tiles.dtype)
    dense = jnp.where(hit[:, :, 0, None, None], tiles[None, :, 0], zero)
    for slot in range(1, row_index.shape[1]):
        dense = dense + jnp.where(hit[:, :, slot, None, None], tiles[None, :, slot], zero)
    return jnp.transpose(dense, (0, 2, 1, 3))


def pick_tiles(dense, row_index):
    feature_blocks = dense.shape[0]
    rows = lax.broadcasted_iota(jnp.int32, (feature_blocks,) + row_index.shape, 0)
    hit = rows == row_index[None]
    by_col = jnp.transpose(dense, (0, 2, 1, 3))
    chosen = jnp.where(hit[:, :, :, None, None], by_col[:, :, None], 0.0)
    return jnp.sum(chosen, axis=0)


def group_size(axis):
    if isinstance(axis, tuple):
        size = 1
        for name in axis:
            size *= lax.axis_size(name)
        return size
    return lax.axis_size(axis)


def butterfly_sum(value, axis):
    size = group_size(axis)
    step = 1
    while step < size:
        value = value + lax.ppermute(value, axis, [(i, i ^ step) for i in range(size)])
        step *= 2
    return value


def gather_rows(value):
    chips = lax.axis_size("chip")
    spread = jnp.broadcast_to(value[None], (chips,) + value.shape)
    mine = lax.all_to_all(spread, "chip", 0, 0, tiled=False)
    other = lax.ppermute(mine, "core", [(0, 1), (1, 0)])
    first = lax.axis_index("core") == 0
    pair = jnp.where(first, jnp.stack([mine, other], 1), jnp.stack([other, mine], 1))
    return pair.reshape((-1,) + value.shape[1:])


def pair_rows(value):
    chips = lax.axis_size("chip")
    parts = value.reshape((chips, 2, -1) + value.shape[1:])
    first = lax.axis_index("core") == 0
    keep = jnp.where(first, parts[:, 0], parts[:, 1])
    give = jnp.where(first, parts[:, 1], parts[:, 0])
    got = lax.ppermute(give, "core", [(0, 1), (1, 0)])
    return (keep.astype(jnp.float32) + got.astype(jnp.float32)).astype(jnp.bfloat16)


def sum_rows(value):
    received = lax.all_to_all(pair_rows(value), "chip", 0, 0, tiled=False)
    return jnp.sum(received.astype(jnp.float32), axis=0)


def split_three(value):
    high = value.astype(jnp.bfloat16)
    rest = value - high.astype(jnp.float32)
    middle = rest.astype(jnp.bfloat16)
    low = (rest - middle.astype(jnp.float32)).astype(jnp.bfloat16)
    return jnp.stack([high, middle, low])


def join_three(pieces):
    pieces = pieces.astype(jnp.float32)
    return pieces[..., 0] + pieces[..., 1] + pieces[..., 2]


def with_row(rows, pieces):
    extra = jnp.zeros((1, rows.shape[1]), rows.dtype).at[0, : pieces.shape[0]].set(pieces)
    return jnp.concatenate([rows, extra], axis=0)


def body(tokens, target, probe_vector, weight_in, weight_out, slot_rows, slot_count):
    columns, unit, slots, block, width_two = weight_in.shape
    features = tokens.shape[1]
    feature_blocks = features // block
    hidden_width = columns * block
    row_index = slot_rows[:, 0]
    in_use = lax.broadcasted_iota(jnp.int32, (columns, slots), 1) < slot_count[:, 0][:, None]
    mask_low = in_use.astype(jnp.bfloat16)[:, :, None, None]
    mask_full = in_use.astype(jnp.float32)[:, :, None, None]
    tiles_in = weight_in[:, 0] * mask_low
    tiles_out = weight_out[:, 0] * mask_low
    chosen = jnp.take(
        probe_vector.reshape(feature_blocks, block), row_index.reshape(-1), axis=0
    ).reshape(columns, slots, block)
    image_part = jnp.einsum(
        "jsk,jskn->jn", chosen, tiles_in.astype(jnp.float32), precision=lax.Precision.HIGHEST
    )
    x_full = gather_rows(tokens)
    image_and_norm = butterfly_sum(
        jnp.concatenate([image_part.reshape(-1), jnp.sum(probe_vector * probe_vector)[None]]), "blk"
    )
    image = image_and_norm[:-1].reshape(image_part.shape)
    norm_probe = image_and_norm[-1]
    norm_image = butterfly_sum(jnp.sum(image * image)[None], WIDE)[0]
    spectral = jnp.sqrt(norm_image / norm_probe)

    w1 = spread_tiles(tiles_in, row_index, feature_blocks).reshape(features, hidden_width)
    w2 = jnp.transpose(
        spread_tiles(tiles_out, row_index, feature_blocks), (2, 1, 0, 3)
    ).reshape(hidden_width, features)

    pre_part = jnp.dot(x_full, w1, preferred_element_type=jnp.float32)
    pre_own = lax.psum_scatter(
        pre_part.astype(jnp.bfloat16), "blk", scatter_dimension=0, tiled=True
    ).astype(jnp.float32)
    pre_own, spectral = lax.optimization_barrier((pre_own, spectral))
    hidden_own = pre_own / spectral
    active_own = activate(hidden_own).astype(jnp.bfloat16)
    active_full = lax.all_gather(active_own, "blk", axis=0, tiled=True)

    out_part = jnp.dot(active_full, w2, preferred_element_type=jnp.float32)
    outputs = sum_rows(out_part.astype(jnp.bfloat16)).astype(jnp.bfloat16)
    residual = (outputs.astype(jnp.float32) - target.astype(jnp.float32)).astype(jnp.bfloat16)
    error_full = gather_rows(residual)

    back_part = lax.dot_general(
        error_full, w2, (((1,), (1,)), ((), ())), preferred_element_type=jnp.float32
    )
    back_own = lax.psum_scatter(
        back_part.astype(jnp.bfloat16), "blk", scatter_dimension=0, tiled=True
    ).astype(jnp.float32)
    g2 = lax.dot_general(
        error_full, active_full, (((0,), (0,)), ((), ())), preferred_element_type=jnp.float32
    )
    grad_out = pick_tiles(g2.reshape(feature_blocks, block, columns, block), row_index) * mask_full
    grad_out = jnp.transpose(grad_out, (0, 1, 3, 2))
    back_own, grad_out = lax.optimization_barrier((back_own, grad_out))
    slope_own = (back_own * activate_slope(hidden_own)).astype(jnp.bfloat16)
    curvature_part = jnp.sum(slope_own.astype(jnp.float32) * pre_own)
    slope_rows = lax.all_gather(
        with_row(slope_own, split_three(curvature_part)), "blk", axis=0, tiled=False
    )
    slope_full = slope_rows[:, :-1].reshape(-1, slope_own.shape[1])
    curvature_blk = jnp.sum(join_three(slope_rows[:, -1, :3]))

    in_part = lax.dot_general(
        slope_full, w1, (((1,), (1,)), ((), ())), preferred_element_type=jnp.float32
    )
    in_rows = pair_rows(in_part.astype(jnp.bfloat16))
    curvature_chip = curvature_blk + lax.ppermute(curvature_blk, "core", [(0, 1), (1, 0)])
    extra = jnp.zeros((in_rows.shape[0], 1, features), jnp.bfloat16).at[:, 0, :3].set(
        split_three(curvature_chip)[None]
    )
    received = lax.all_to_all(
        jnp.concatenate([in_rows, extra], axis=1), "chip", 0, 0, tiled=False
    )
    token_grad = (
        jnp.sum(received[:, :-1].astype(jnp.float32), axis=0) / spectral
    ).astype(jnp.bfloat16)
    curvature = jnp.sum(join_three(received[:, -1, :3]))

    g1 = lax.dot_general(
        x_full, slope_full, (((0,), (0,)), ((), ())), preferred_element_type=jnp.float32
    )
    raw_in = pick_tiles(g1.reshape(feature_blocks, block, columns, block), row_index) * mask_full

    outer = jnp.einsum("jsk,jn->jskn", chosen, image) * mask_full
    grad_in = raw_in / spectral - curvature / (spectral**3 * norm_probe) * outer
    return (outputs, token_grad, grad_in[:, None], grad_out[:, None])


def solution(mesh):
    wide, blk = mesh.shape["wide"], mesh.shape["blk"]
    split = Mesh(mesh.devices.reshape(wide // 2, 2, blk), ("chip", "core", "blk"))
    in_specs = (
        P(WIDE, "blk"),
        P(WIDE, "blk"),
        P("blk"),
        P(WIDE, "blk", None, None, None),
        P(WIDE, "blk", None, None, None),
        P(WIDE, "blk", None),
        P(WIDE, "blk"),
    )
    out_specs = (
        P(WIDE, "blk"),
        P(WIDE, "blk"),
        P(WIDE, "blk", None, None, None),
        P(WIDE, "blk", None, None, None),
    )
    return jax.shard_map(body, mesh=split, in_specs=in_specs, out_specs=out_specs, check_vma=False)
```

```python
import jax
import jax.numpy as jnp
from jax import lax
from jax.sharding import Mesh, PartitionSpec as P

WIDE = ("chip", "core")


def activate(value):
    return jax.nn.gelu(value, approximate=True)


def activate_slope(value):
    return jax.jvp(activate, (value,), (jnp.ones_like(value),))[1]


def spread_tiles(tiles, row_index, feature_blocks):
    rows = lax.broadcasted_iota(jnp.int32, (feature_blocks,) + row_index.shape, 0)
    hit = rows == row_index[None]
    zero = jnp.zeros((), tiles.dtype)
    dense = jnp.where(hit[:, :, 0, None, None], tiles[None, :, 0], zero)
    for slot in range(1, row_index.shape[1]):
        dense = dense + jnp.where(hit[:, :, slot, None, None], tiles[None, :, slot], zero)
    return jnp.transpose(dense, (0, 2, 1, 3))


def pick_tiles(dense, row_index):
    feature_blocks = dense.shape[0]
    rows = lax.broadcasted_iota(jnp.int32, (feature_blocks,) + row_index.shape, 0)
    hit = rows == row_index[None]
    by_col = jnp.transpose(dense, (0, 2, 1, 3))
    chosen = jnp.where(hit[:, :, :, None, None], by_col[:, :, None], 0.0)
    return jnp.sum(chosen, axis=0)


def group_size(axis):
    if isinstance(axis, tuple):
        size = 1
        for name in axis:
            size *= lax.axis_size(name)
        return size
    return lax.axis_size(axis)


def butterfly_sum(value, axis):
    size = group_size(axis)
    step = 1
    while step < size:
        value = value + lax.ppermute(value, axis, [(i, i ^ step) for i in range(size)])
        step *= 2
    return value


def gather_rows(value):
    chips = lax.axis_size("chip")
    spread = jnp.broadcast_to(value[None], (chips,) + value.shape)
    mine = lax.all_to_all(spread, "chip", 0, 0, tiled=False)
    other = lax.ppermute(mine, "core", [(0, 1), (1, 0)])
    first = lax.axis_index("core") == 0
    pair = jnp.stack([jnp.where(first, mine, other), jnp.where(first, other, mine)], 1)
    return pair.reshape((-1,) + value.shape[1:])


def pair_rows(value):
    chips = lax.axis_size("chip")
    parts = value.reshape((chips, 2, -1) + value.shape[1:])
    first = lax.axis_index("core") == 0
    keep = jnp.where(first, parts[:, 0], parts[:, 1])
    give = jnp.where(first, parts[:, 1], parts[:, 0])
    got = lax.ppermute(give, "core", [(0, 1), (1, 0)])
    return (keep.astype(jnp.float32) + got.astype(jnp.float32)).astype(jnp.bfloat16)


def sum_rows(value):
    received = lax.all_to_all(pair_rows(value), "chip", 0, 0, tiled=False)
    return jnp.sum(received.astype(jnp.float32), axis=0)


def split_three(value):
    high = value.astype(jnp.bfloat16)
    rest = value - high.astype(jnp.float32)
    middle = rest.astype(jnp.bfloat16)
    low = (rest - middle.astype(jnp.float32)).astype(jnp.bfloat16)
    return jnp.stack([high, middle, low])


def join_three(pieces):
    pieces = pieces.astype(jnp.float32)
    return pieces[..., 0] + pieces[..., 1] + pieces[..., 2]


def with_row(rows, pieces):
    extra = jnp.zeros((1, rows.shape[1]), rows.dtype).at[0, : pieces.shape[0]].set(pieces)
    return jnp.concatenate([rows, extra], axis=0)


def body(tokens, target, probe_vector, weight_in, weight_out, slot_rows, slot_count):
    columns, unit, slots, block, width_two = weight_in.shape
    features = tokens.shape[1]
    feature_blocks = features // block
    hidden_width = columns * block
    row_index = slot_rows[:, 0]
    in_use = lax.broadcasted_iota(jnp.int32, (columns, slots), 1) < slot_count[:, 0][:, None]
    mask_low = in_use.astype(jnp.bfloat16)[:, :, None, None]
    mask_full = in_use.astype(jnp.float32)[:, :, None, None]
    tiles_in = weight_in[:, 0] * mask_low
    tiles_out = weight_out[:, 0] * mask_low
    chosen = jnp.take(
        probe_vector.reshape(feature_blocks, block), row_index.reshape(-1), axis=0
    ).reshape(columns, slots, block)
    image_part = jnp.einsum(
        "jsk,jskn->jn", chosen, tiles_in.astype(jnp.float32), precision=lax.Precision.HIGHEST
    )
    x_full = gather_rows(tokens)
    image_and_norm = butterfly_sum(
        jnp.concatenate([image_part.reshape(-1), jnp.sum(probe_vector * probe_vector)[None]]), "blk"
    )
    image = image_and_norm[:-1].reshape(image_part.shape)
    norm_probe = image_and_norm[-1]
    norm_image = butterfly_sum(jnp.sum(image * image)[None], WIDE)[0]
    spectral = jnp.sqrt(norm_image / norm_probe)

    w1 = spread_tiles(tiles_in, row_index, feature_blocks).reshape(features, hidden_width)
    w2 = jnp.transpose(
        spread_tiles(tiles_out, row_index, feature_blocks), (2, 1, 0, 3)
    ).reshape(hidden_width, features)

    pre_part = jnp.dot(x_full, w1, preferred_element_type=jnp.float32)
    pre_own = lax.psum_scatter(
        pre_part.astype(jnp.bfloat16), "blk", scatter_dimension=0, tiled=True
    ).astype(jnp.float32)
    pre_own, spectral = lax.optimization_barrier((pre_own, spectral))
    hidden_own = pre_own / spectral
    active_own = activate(hidden_own).astype(jnp.bfloat16)
    active_full = lax.all_gather(active_own, "blk", axis=0, tiled=True)

    out_part = jnp.dot(active_full, w2, preferred_element_type=jnp.float32)
    outputs = sum_rows(out_part.astype(jnp.bfloat16)).astype(jnp.bfloat16)
    residual = (outputs.astype(jnp.float32) - target.astype(jnp.float32)).astype(jnp.bfloat16)
    error_full = gather_rows(residual)

    back_part = lax.dot_general(
        error_full, w2, (((1,), (1,)), ((), ())), preferred_element_type=jnp.float32
    )
    back_own = lax.psum_scatter(
        back_part.astype(jnp.bfloat16), "blk", scatter_dimension=0, tiled=True
    ).astype(jnp.float32)
    g2 = lax.dot_general(
        error_full, active_full, (((0,), (0,)), ((), ())), preferred_element_type=jnp.float32
    )
    grad_out = pick_tiles(g2.reshape(feature_blocks, block, columns, block), row_index) * mask_full
    grad_out = jnp.transpose(grad_out, (0, 1, 3, 2))
    back_own, grad_out = lax.optimization_barrier((back_own, grad_out))
    slope_own = (back_own * activate_slope(hidden_own)).astype(jnp.bfloat16)
    curvature_part = jnp.sum(slope_own.astype(jnp.float32) * pre_own)
    slope_rows = lax.all_gather(
        with_row(slope_own, split_three(curvature_part)), "blk", axis=0, tiled=False
    )
    slope_full = slope_rows[:, :-1].reshape(-1, slope_own.shape[1])
    curvature_blk = jnp.sum(join_three(slope_rows[:, -1, :3]))

    in_part = lax.dot_general(
        slope_full, w1, (((1,), (1,)), ((), ())), preferred_element_type=jnp.float32
    )
    in_rows = pair_rows(in_part.astype(jnp.bfloat16))
    curvature_chip = curvature_blk + lax.ppermute(curvature_blk, "core", [(0, 1), (1, 0)])
    extra = jnp.zeros((in_rows.shape[0], 1, features), jnp.bfloat16).at[:, 0, :3].set(
        split_three(curvature_chip)[None]
    )
    received = lax.all_to_all(
        jnp.concatenate([in_rows, extra], axis=1), "chip", 0, 0, tiled=False
    )
    token_grad = (
        jnp.sum(received[:, :-1].astype(jnp.float32), axis=0) / spectral
    ).astype(jnp.bfloat16)
    curvature = jnp.sum(join_three(received[:, -1, :3]))

    g1 = lax.dot_general(
        x_full, slope_full, (((0,), (0,)), ((), ())), preferred_element_type=jnp.float32
    )
    raw_in = pick_tiles(g1.reshape(feature_blocks, block, columns, block), row_index) * mask_full

    outer = jnp.einsum("jsk,jn->jskn", chosen, image) * mask_full
    grad_in = raw_in / spectral - curvature / (spectral**3 * norm_probe) * outer
    return (outputs, token_grad, grad_in[:, None], grad_out[:, None])


def solution(mesh):
    wide, blk = mesh.shape["wide"], mesh.shape["blk"]
    split = Mesh(mesh.devices.reshape(wide // 2, 2, blk), ("chip", "core", "blk"))
    in_specs = (
        P(WIDE, "blk"),
        P(WIDE, "blk"),
        P("blk"),
        P(WIDE, "blk", None, None, None),
        P(WIDE, "blk", None, None, None),
        P(WIDE, "blk", None),
        P(WIDE, "blk"),
    )
    out_specs = (
        P(WIDE, "blk"),
        P(WIDE, "blk"),
        P(WIDE, "blk", None, None, None),
        P(WIDE, "blk", None, None, None),
    )
    return jax.shard_map(body, mesh=split, in_specs=in_specs, out_specs=out_specs, check_vma=False)
```

```python
import jax
import jax.numpy as jnp
from jax import lax
from jax.sharding import Mesh, PartitionSpec as P

WIDE = ("chip", "core")


def activate(value):
    return jax.nn.gelu(value, approximate=True)


def activate_slope(value):
    return jax.jvp(activate, (value,), (jnp.ones_like(value),))[1]


def spread_tiles(tiles, row_index, feature_blocks):
    rows = lax.broadcasted_iota(jnp.int32, (feature_blocks,) + row_index.shape, 0)
    hit = rows == row_index[None]
    zero = jnp.zeros((), tiles.dtype)
    dense = jnp.where(hit[:, :, 0, None, None], tiles[None, :, 0], zero)
    for slot in range(1, row_index.shape[1]):
        dense = dense + jnp.where(hit[:, :, slot, None, None], tiles[None, :, slot], zero)
    return jnp.transpose(dense, (0, 2, 1, 3))


def pick_tiles(dense, row_index):
    feature_blocks = dense.shape[0]
    rows = lax.broadcasted_iota(jnp.int32, (feature_blocks,) + row_index.shape, 0)
    hit = rows == row_index[None]
    by_col = jnp.transpose(dense, (0, 2, 1, 3))
    chosen = jnp.where(hit[:, :, :, None, None], by_col[:, :, None], 0.0)
    return jnp.sum(chosen, axis=0)


def group_size(axis):
    if isinstance(axis, tuple):
        size = 1
        for name in axis:
            size *= lax.axis_size(name)
        return size
    return lax.axis_size(axis)


def butterfly_sum(value, axis):
    size = group_size(axis)
    step = 1
    while step < size:
        value = value + lax.ppermute(value, axis, [(i, i ^ step) for i in range(size)])
        step *= 2
    return value


def gather_rows(value):
    chips = lax.axis_size("chip")
    spread = jnp.broadcast_to(value[None], (chips,) + value.shape)
    mine = lax.all_to_all(spread, "chip", 0, 0, tiled=False)
    other = lax.ppermute(mine, "core", [(0, 1), (1, 0)])
    first = lax.axis_index("core") == 0
    pair = jnp.stack([jnp.where(first, mine, other), jnp.where(first, other, mine)], 1)
    return pair.reshape((-1,) + value.shape[1:])


def pair_rows(left, product):
    chips = lax.axis_size("chip")
    parts = left.reshape((chips, 2, -1) + left.shape[1:])
    first = lax.axis_index("core") == 0
    keep_in = jnp.where(first, parts[:, 0], parts[:, 1]).reshape((-1,) + left.shape[1:])
    give_in = jnp.where(first, parts[:, 1], parts[:, 0]).reshape((-1,) + left.shape[1:])
    give = product(give_in).astype(jnp.bfloat16)
    got = lax.ppermute(give, "core", [(0, 1), (1, 0)])
    keep = product(keep_in).astype(jnp.bfloat16)
    pair = keep.astype(jnp.float32) + got.astype(jnp.float32)
    return pair.astype(jnp.bfloat16).reshape((chips, -1) + pair.shape[1:])


def sum_rows(left, product):
    received = lax.all_to_all(pair_rows(left, product), "chip", 0, 0, tiled=False)
    return jnp.sum(received.astype(jnp.float32), axis=0)


def split_three(value):
    high = value.astype(jnp.bfloat16)
    rest = value - high.astype(jnp.float32)
    middle = rest.astype(jnp.bfloat16)
    low = (rest - middle.astype(jnp.float32)).astype(jnp.bfloat16)
    return jnp.stack([high, middle, low])


def join_three(pieces):
    pieces = pieces.astype(jnp.float32)
    return pieces[..., 0] + pieces[..., 1] + pieces[..., 2]


def with_row(rows, pieces):
    extra = jnp.zeros((1, rows.shape[1]), rows.dtype).at[0, : pieces.shape[0]].set(pieces)
    return jnp.concatenate([rows, extra], axis=0)


def body(tokens, target, probe_vector, weight_in, weight_out, slot_rows, slot_count):
    columns, unit, slots, block, width_two = weight_in.shape
    features = tokens.shape[1]
    feature_blocks = features // block
    hidden_width = columns * block
    row_index = slot_rows[:, 0]
    in_use = lax.broadcasted_iota(jnp.int32, (columns, slots), 1) < slot_count[:, 0][:, None]
    mask_low = in_use.astype(jnp.bfloat16)[:, :, None, None]
    mask_full = in_use.astype(jnp.float32)[:, :, None, None]
    tiles_in = weight_in[:, 0] * mask_low
    tiles_out = weight_out[:, 0] * mask_low
    chosen = jnp.take(
        probe_vector.reshape(feature_blocks, block), row_index.reshape(-1), axis=0
    ).reshape(columns, slots, block)
    image_part = jnp.einsum(
        "jsk,jskn->jn", chosen, tiles_in.astype(jnp.float32), precision=lax.Precision.HIGHEST
    )
    x_full = gather_rows(tokens)
    image_and_norm = butterfly_sum(
        jnp.concatenate([image_part.reshape(-1), jnp.sum(probe_vector * probe_vector)[None]]), "blk"
    )
    image = image_and_norm[:-1].reshape(image_part.shape)
    norm_probe = image_and_norm[-1]
    norm_image = butterfly_sum(jnp.sum(image * image)[None], WIDE)[0]
    spectral = jnp.sqrt(norm_image / norm_probe)

    w1 = spread_tiles(tiles_in, row_index, feature_blocks).reshape(features, hidden_width)
    w2 = jnp.transpose(
        spread_tiles(tiles_out, row_index, feature_blocks), (2, 1, 0, 3)
    ).reshape(hidden_width, features)

    pre_part = jnp.dot(x_full, w1, preferred_element_type=jnp.float32)
    pre_own = lax.psum_scatter(
        pre_part.astype(jnp.bfloat16), "blk", scatter_dimension=0, tiled=True
    ).astype(jnp.float32)
    pre_own, spectral = lax.optimization_barrier((pre_own, spectral))
    hidden_own = pre_own / spectral
    active_own = activate(hidden_own).astype(jnp.bfloat16)
    active_full = lax.all_gather(active_own, "blk", axis=0, tiled=True)

    outputs = sum_rows(
        active_full, lambda rows: jnp.dot(rows, w2, preferred_element_type=jnp.float32)
    ).astype(jnp.bfloat16)
    residual = (outputs.astype(jnp.float32) - target.astype(jnp.float32)).astype(jnp.bfloat16)
    error_full = gather_rows(residual)

    back_part = lax.dot_general(
        error_full, w2, (((1,), (1,)), ((), ())), preferred_element_type=jnp.float32
    )
    back_own = lax.psum_scatter(
        back_part.astype(jnp.bfloat16), "blk", scatter_dimension=0, tiled=True
    ).astype(jnp.float32)
    g2 = lax.dot_general(
        error_full, active_full, (((0,), (0,)), ((), ())), preferred_element_type=jnp.float32
    )
    grad_out = pick_tiles(g2.reshape(feature_blocks, block, columns, block), row_index) * mask_full
    grad_out = jnp.transpose(grad_out, (0, 1, 3, 2))
    back_own, grad_out = lax.optimization_barrier((back_own, grad_out))
    slope_own = (back_own * activate_slope(hidden_own)).astype(jnp.bfloat16)
    curvature_part = jnp.sum(slope_own.astype(jnp.float32) * pre_own)
    slope_rows = lax.all_gather(
        with_row(slope_own, split_three(curvature_part)), "blk", axis=0, tiled=False
    )
    slope_full = slope_rows[:, :-1].reshape(-1, slope_own.shape[1])
    curvature_blk = jnp.sum(join_three(slope_rows[:, -1, :3]))

    in_rows = pair_rows(
        slope_full,
        lambda rows: lax.dot_general(
            rows, w1, (((1,), (1,)), ((), ())), preferred_element_type=jnp.float32
        ),
    )
    curvature_chip = curvature_blk + lax.ppermute(curvature_blk, "core", [(0, 1), (1, 0)])
    extra = jnp.zeros((in_rows.shape[0], 1, features), jnp.bfloat16).at[:, 0, :3].set(
        split_three(curvature_chip)[None]
    )
    received = lax.all_to_all(
        jnp.concatenate([in_rows, extra], axis=1), "chip", 0, 0, tiled=False
    )
    token_grad = (
        jnp.sum(received[:, :-1].astype(jnp.float32), axis=0) / spectral
    ).astype(jnp.bfloat16)
    curvature = jnp.sum(join_three(received[:, -1, :3]))

    g1 = lax.dot_general(
        x_full, slope_full, (((0,), (0,)), ((), ())), preferred_element_type=jnp.float32
    )
    raw_in = pick_tiles(g1.reshape(feature_blocks, block, columns, block), row_index) * mask_full

    outer = jnp.einsum("jsk,jn->jskn", chosen, image) * mask_full
    grad_in = raw_in / spectral - curvature / (spectral**3 * norm_probe) * outer
    return (outputs, token_grad, grad_in[:, None], grad_out[:, None])


def solution(mesh):
    wide, blk = mesh.shape["wide"], mesh.shape["blk"]
    split = Mesh(mesh.devices.reshape(wide // 2, 2, blk), ("chip", "core", "blk"))
    in_specs = (
        P(WIDE, "blk"),
        P(WIDE, "blk"),
        P("blk"),
        P(WIDE, "blk", None, None, None),
        P(WIDE, "blk", None, None, None),
        P(WIDE, "blk", None),
        P(WIDE, "blk"),
    )
    out_specs = (
        P(WIDE, "blk"),
        P(WIDE, "blk"),
        P(WIDE, "blk", None, None, None),
        P(WIDE, "blk", None, None, None),
    )
    return jax.shard_map(body, mesh=split, in_specs=in_specs, out_specs=out_specs, check_vma=False)
```

```python
import jax
import jax.numpy as jnp
from jax import lax
from jax.sharding import Mesh, PartitionSpec as P

WIDE = ("chip", "core")


def activate(value):
    return jax.nn.gelu(value, approximate=True)


def activate_slope(value):
    return jax.jvp(activate, (value,), (jnp.ones_like(value),))[1]


def spread_tiles(tiles, row_index, feature_blocks):
    rows = lax.broadcasted_iota(jnp.int32, (feature_blocks,) + row_index.shape, 0)
    hit = rows == row_index[None]
    zero = jnp.zeros((), tiles.dtype)
    dense = jnp.where(hit[:, :, 0, None, None], tiles[None, :, 0], zero)
    for slot in range(1, row_index.shape[1]):
        dense = dense + jnp.where(hit[:, :, slot, None, None], tiles[None, :, slot], zero)
    return jnp.transpose(dense, (0, 2, 1, 3))


def pick_tiles(dense, row_index):
    feature_blocks = dense.shape[0]
    rows = lax.broadcasted_iota(jnp.int32, (feature_blocks,) + row_index.shape, 0)
    hit = rows == row_index[None]
    by_col = jnp.transpose(dense, (0, 2, 1, 3))
    chosen = jnp.where(hit[:, :, :, None, None], by_col[:, :, None], 0.0)
    return jnp.sum(chosen, axis=0)


def group_size(axis):
    if isinstance(axis, tuple):
        size = 1
        for name in axis:
            size *= lax.axis_size(name)
        return size
    return lax.axis_size(axis)


def butterfly_sum(value, axis):
    size = group_size(axis)
    step = 1
    while step < size:
        value = value + lax.ppermute(value, axis, [(i, i ^ step) for i in range(size)])
        step *= 2
    return value


def gather_rows(value):
    chips = lax.axis_size("chip")
    spread = jnp.broadcast_to(value[None], (chips,) + value.shape)
    mine = lax.all_to_all(spread, "chip", 0, 0, tiled=False)
    other = lax.ppermute(mine, "core", [(0, 1), (1, 0)])
    first = lax.axis_index("core") == 0
    pair = jnp.stack([jnp.where(first, mine, other), jnp.where(first, other, mine)], 1)
    return pair.reshape((-1,) + value.shape[1:])


def gather_halves(value):
    chips = lax.axis_size("chip")
    spread = jnp.broadcast_to(value[None], (chips,) + value.shape)
    mine = lax.all_to_all(spread, "chip", 0, 0, tiled=False)
    other = lax.ppermute(mine, "core", [(0, 1), (1, 0)])
    return mine, other


def order_pair(mine, other):
    first = lax.axis_index("core") == 0
    pair = jnp.stack([jnp.where(first, mine, other), jnp.where(first, other, mine)], 1)
    return pair.reshape((-1,) + mine.shape[2:])


def pair_rows(left, product):
    chips = lax.axis_size("chip")
    parts = left.reshape((chips, 2, -1) + left.shape[1:])
    first = lax.axis_index("core") == 0
    keep_in = jnp.where(first, parts[:, 0], parts[:, 1]).reshape((-1,) + left.shape[1:])
    give_in = jnp.where(first, parts[:, 1], parts[:, 0]).reshape((-1,) + left.shape[1:])
    give = product(give_in).astype(jnp.bfloat16)
    got = lax.ppermute(give, "core", [(0, 1), (1, 0)])
    keep = product(keep_in).astype(jnp.bfloat16)
    pair = keep.astype(jnp.float32) + got.astype(jnp.float32)
    return pair.astype(jnp.bfloat16).reshape((chips, -1) + pair.shape[1:])


def sum_rows(left, product):
    received = lax.all_to_all(pair_rows(left, product), "chip", 0, 0, tiled=False)
    return jnp.sum(received.astype(jnp.float32), axis=0)


def split_three(value):
    high = value.astype(jnp.bfloat16)
    rest = value - high.astype(jnp.float32)
    middle = rest.astype(jnp.bfloat16)
    low = (rest - middle.astype(jnp.float32)).astype(jnp.bfloat16)
    return jnp.stack([high, middle, low])


def join_three(pieces):
    pieces = pieces.astype(jnp.float32)
    return pieces[..., 0] + pieces[..., 1] + pieces[..., 2]


def with_row(rows, pieces):
    extra = jnp.zeros((1, rows.shape[1]), rows.dtype).at[0, : pieces.shape[0]].set(pieces)
    return jnp.concatenate([rows, extra], axis=0)


def body(tokens, target, probe_vector, weight_in, weight_out, slot_rows, slot_count):
    columns, unit, slots, block, width_two = weight_in.shape
    features = tokens.shape[1]
    feature_blocks = features // block
    hidden_width = columns * block
    row_index = slot_rows[:, 0]
    in_use = lax.broadcasted_iota(jnp.int32, (columns, slots), 1) < slot_count[:, 0][:, None]
    mask_low = in_use.astype(jnp.bfloat16)[:, :, None, None]
    mask_full = in_use.astype(jnp.float32)[:, :, None, None]
    tiles_in = weight_in[:, 0] * mask_low
    tiles_out = weight_out[:, 0] * mask_low
    chosen = jnp.take(
        probe_vector.reshape(feature_blocks, block), row_index.reshape(-1), axis=0
    ).reshape(columns, slots, block)
    image_part = jnp.einsum(
        "jsk,jskn->jn", chosen, tiles_in.astype(jnp.float32), precision=lax.Precision.HIGHEST
    )
    x_mine, x_other = gather_halves(tokens)
    x_full = order_pair(x_mine, x_other)
    image_and_norm = butterfly_sum(
        jnp.concatenate([image_part.reshape(-1), jnp.sum(probe_vector * probe_vector)[None]]), "blk"
    )
    image = image_and_norm[:-1].reshape(image_part.shape)
    norm_probe = image_and_norm[-1]
    norm_image = butterfly_sum(jnp.sum(image * image)[None], WIDE)[0]
    spectral = jnp.sqrt(norm_image / norm_probe)

    w1 = spread_tiles(tiles_in, row_index, feature_blocks).reshape(features, hidden_width)
    w2 = jnp.transpose(
        spread_tiles(tiles_out, row_index, feature_blocks), (2, 1, 0, 3)
    ).reshape(hidden_width, features)

    pre_mine = jnp.dot(x_mine, w1, preferred_element_type=jnp.float32)
    pre_other = jnp.dot(x_other, w1, preferred_element_type=jnp.float32)
    pre_part = order_pair(pre_mine, pre_other)
    pre_own = lax.psum_scatter(
        pre_part.astype(jnp.bfloat16), "blk", scatter_dimension=0, tiled=True
    ).astype(jnp.float32)
    pre_own, spectral = lax.optimization_barrier((pre_own, spectral))
    hidden_own = pre_own / spectral
    active_own = activate(hidden_own).astype(jnp.bfloat16)
    active_full = lax.all_gather(active_own, "blk", axis=0, tiled=True)

    outputs = sum_rows(
        active_full, lambda rows: jnp.dot(rows, w2, preferred_element_type=jnp.float32)
    ).astype(jnp.bfloat16)
    residual = (outputs.astype(jnp.float32) - target.astype(jnp.float32)).astype(jnp.bfloat16)
    error_full = gather_rows(residual)

    back_part = lax.dot_general(
        error_full, w2, (((1,), (1,)), ((), ())), preferred_element_type=jnp.float32
    )
    back_own = lax.psum_scatter(
        back_part.astype(jnp.bfloat16), "blk", scatter_dimension=0, tiled=True
    ).astype(jnp.float32)
    g2 = lax.dot_general(
        error_full, active_full, (((0,), (0,)), ((), ())), preferred_element_type=jnp.float32
    )
    grad_out = pick_tiles(g2.reshape(feature_blocks, block, columns, block), row_index) * mask_full
    grad_out = jnp.transpose(grad_out, (0, 1, 3, 2))
    back_own, grad_out = lax.optimization_barrier((back_own, grad_out))
    slope_own = (back_own * activate_slope(hidden_own)).astype(jnp.bfloat16)
    curvature_part = jnp.sum(slope_own.astype(jnp.float32) * pre_own)
    slope_rows = lax.all_gather(
        with_row(slope_own, split_three(curvature_part)), "blk", axis=0, tiled=False
    )
    slope_full = slope_rows[:, :-1].reshape(-1, slope_own.shape[1])
    curvature_blk = jnp.sum(join_three(slope_rows[:, -1, :3]))

    in_rows = pair_rows(
        slope_full,
        lambda rows: lax.dot_general(
            rows, w1, (((1,), (1,)), ((), ())), preferred_element_type=jnp.float32
        ),
    )
    curvature_chip = curvature_blk + lax.ppermute(curvature_blk, "core", [(0, 1), (1, 0)])
    extra = jnp.zeros((in_rows.shape[0], 1, features), jnp.bfloat16).at[:, 0, :3].set(
        split_three(curvature_chip)[None]
    )
    received = lax.all_to_all(
        jnp.concatenate([in_rows, extra], axis=1), "chip", 0, 0, tiled=False
    )
    token_grad = (
        jnp.sum(received[:, :-1].astype(jnp.float32), axis=0) / spectral
    ).astype(jnp.bfloat16)
    curvature = jnp.sum(join_three(received[:, -1, :3]))

    g1 = lax.dot_general(
        x_full, slope_full, (((0,), (0,)), ((), ())), preferred_element_type=jnp.float32
    )
    raw_in = pick_tiles(g1.reshape(feature_blocks, block, columns, block), row_index) * mask_full

    outer = jnp.einsum("jsk,jn->jskn", chosen, image) * mask_full
    grad_in = raw_in / spectral - curvature / (spectral**3 * norm_probe) * outer
    return (outputs, token_grad, grad_in[:, None], grad_out[:, None])


def solution(mesh):
    wide, blk = mesh.shape["wide"], mesh.shape["blk"]
    split = Mesh(mesh.devices.reshape(wide // 2, 2, blk), ("chip", "core", "blk"))
    in_specs = (
        P(WIDE, "blk"),
        P(WIDE, "blk"),
        P("blk"),
        P(WIDE, "blk", None, None, None),
        P(WIDE, "blk", None, None, None),
        P(WIDE, "blk", None),
        P(WIDE, "blk"),
    )
    out_specs = (
        P(WIDE, "blk"),
        P(WIDE, "blk"),
        P(WIDE, "blk", None, None, None),
        P(WIDE, "blk", None, None, None),
    )
    return jax.shard_map(body, mesh=split, in_specs=in_specs, out_specs=out_specs, check_vma=False)
```
